256 devices in a mesh: row: 8 (over z), col: 32 (over y, x, core).
Axes of the slice: x: 4, y: 4, z: 8, core: 2. Of those that a mesh axis runs over, the one named last changes fastest.
Arguments:
- tokens: bfloat16 [512, 8192], P('col', 'row'), may hold values from -6 to 6
- cotangent: bfloat16 [512, 8192], P('col', 'row'), may hold values from -6 to 6
- w_gate: bfloat16 [8192, 16384], P('row', 'col'), may hold values from -0.09375 to 0.09375
- w_up: bfloat16 [8192, 16384], P('row', 'col'), may hold values from -0.09375 to 0.09375
- w_down: bfloat16 [16384, 8192], P('col', 'row'), may hold values from -0.0625 to 0.0625
- order_gate: int32 [2048], replicated, may hold values from 0 to 2047, each once
- order_up: int32 [2048], replicated, may hold values from 0 to 2047, each once
- order_down: int32 [2048], replicated, may hold values from 0 to 2047, each once
Outputs:
- output: bfloat16 [512, 8192], P('col', 'row')
- input_grad: bfloat16 [512, 8192], P('col', 'row')
- gate_weight_grad: float32 [8192, 16384], P('row', 'col')
- up_weight_grad: float32 [8192, 16384], P('row', 'col')
- down_weight_grad: float32 [16384, 8192], P('col', 'row')
The draws below stay inside these ranges and needn't reach their ends.
Inputs may be any that keep to these rules, and one draw needn't show every extreme that they name: `order_gate`: each of the 2048 block numbers appears exactly once. `order_up`: each of the 2048 block numbers appears exactly once. `order_down`: each of the 2048 block numbers appears exactly once.
All inputs are finite; a program needn't handle non-finite values.
Results may differ from the reference program's by a relative error of at most 0.0049.
Values may be sent and summed in bfloat16 or wider, within the bound.
No kernel may reach another device: no remote copies, remote signals or barrier semaphores. Data moves between devices by JAX's collectives and lax.ppermute only.
A program may use at most 64 MiB of HBM per device.

```python
import jax
import jax.numpy as jnp

D = 8192
FF = 16384
BLOCK = 256
TOKENS = 512
DB = 32
FB = 64
NB = 2048
KEPT = 1024


def levels(own_key, dims, pieces, low, high):
    def one(position, shards_of):
        draws = jax.random.uniform(jax.random.fold_in(jax.random.fold_in(own_key, 6), position), (shards_of,), jnp.float32, low / len(pieces), high / len(pieces))
        return jnp.repeat(jnp.exp(draws), dims[position] // shards_of).reshape((-1,) + (1,) * (len(dims) - position - 1))

    level = one(*pieces[0])
    for cut in pieces[1:]:
        level = level * one(*cut)
    return level


def centred(key, dims, scale, reach, cuts=(), held_as=jnp.bfloat16):
    result = jax.random.normal(key, dims, jnp.float32) * scale
    if len(cuts) > 0:
        result = levels(key, dims, cuts, -0.22, 0.18) * result
    return jnp.clip(result, min=-reach, max=reach).astype(held_as)


def setup_inputs(seed: int = 0) -> dict:
    keys = jax.random.split(jax.random.key(seed), 9)
    tokens = centred(keys[0], (TOKENS, D), 1.0, 6.0, ((0, 32), (1, 8)))
    cotangent = centred(keys[1], (TOKENS, D), 1.0, 6.0, ((0, 32), (1, 8)))
    w_gate = centred(keys[2], (D, FF), (D // 2) ** -0.5, 0.09375, ((0, 8), (1, 32)))
    w_up = centred(keys[3], (D, FF), (D // 2) ** -0.5, 0.09375, ((0, 8), (1, 32)))
    w_down = centred(keys[4], (FF, D), (FF // 2) ** -0.5, 0.0625, ((0, 32), (1, 8)))
    order_gate = jax.random.permutation(keys[5], NB).astype(jnp.int32)
    order_up = jax.random.permutation(keys[6], NB).astype(jnp.int32)
    order_down = jax.random.permutation(keys[7], NB).astype(jnp.int32)
    return {"tokens": tokens, "cotangent": cotangent, "w_gate": w_gate, "w_up": w_up, "w_down": w_down, "order_gate": order_gate, "order_up": order_up, "order_down": order_down}


def block_mask(order, rows_blocks, cols_blocks):
    total = rows_blocks * cols_blocks
    ranks = jnp.zeros((total,), jnp.int32).at[order].set(jnp.arange(total, dtype=jnp.int32))
    kept_mask = (ranks < KEPT).reshape(rows_blocks, cols_blocks)
    full_mask = jnp.repeat(jnp.repeat(kept_mask, BLOCK, axis=0), BLOCK, axis=1)
    return full_mask.astype(jnp.bfloat16)


def reference(tokens, cotangent, w_gate, w_up, w_down, order_gate, order_up, order_down):
    mask_gate = block_mask(order_gate, DB, FB)
    mask_up = block_mask(order_up, DB, FB)
    mask_down = block_mask(order_down, FB, DB)
    gate_kept = w_gate * mask_gate
    up_kept = w_up * mask_up
    down_kept = w_down * mask_down
    gate = jnp.dot(tokens, gate_kept, preferred_element_type=jnp.float32)
    up = jnp.dot(tokens, up_kept, preferred_element_type=jnp.float32)
    sigmoid_gate = jax.nn.sigmoid(gate)
    activation = gate * sigmoid_gate
    hidden = (activation * up).astype(jnp.bfloat16)
    output = jnp.dot(hidden, down_kept, preferred_element_type=jnp.float32).astype(jnp.bfloat16)
    hidden_grad = jnp.dot(cotangent, down_kept.T, preferred_element_type=jnp.float32)
    gate_grad = (hidden_grad * up * sigmoid_gate * (1.0 + gate * (1.0 - sigmoid_gate))).astype(jnp.bfloat16)
    up_grad = (hidden_grad * activation).astype(jnp.bfloat16)
    down_weight_grad = jnp.dot(hidden.T, cotangent, preferred_element_type=jnp.float32) * mask_down.astype(jnp.float32)
    gate_weight_grad = jnp.dot(tokens.T, gate_grad, preferred_element_type=jnp.float32) * mask_gate.astype(jnp.float32)
    up_weight_grad = jnp.dot(tokens.T, up_grad, preferred_element_type=jnp.float32) * mask_up.astype(jnp.float32)
    through_gate = jnp.dot(gate_grad, gate_kept.T, preferred_element_type=jnp.float32)
    through_up = jnp.dot(up_grad, up_kept.T, preferred_element_type=jnp.float32)
    input_grad = (through_gate + through_up).astype(jnp.bfloat16)
    return (output, input_grad, gate_weight_grad, up_weight_grad, down_weight_grad)
```

```python
import jax
import jax.numpy as jnp
from jax import lax
from jax.sharding import PartitionSpec as P

BLOCK = 256


def kept_table(order, row_first, col_first, row_count, col_count, stride):
    kept_count = order.shape[0] // 2
    row_ids = row_first + jnp.arange(row_count, dtype=jnp.int32)
    col_ids = col_first + jnp.arange(col_count, dtype=jnp.int32)
    block_ids = row_ids[:, None] * stride + col_ids[None, :]
    return jnp.any(block_ids[:, :, None] == order[:kept_count][None, None, :], axis=2)


def expand_mask(kept_mask):
    row_count, col_count = kept_mask.shape
    spread = jnp.broadcast_to(kept_mask[:, None, :, None], (row_count, BLOCK, col_count, BLOCK))
    return spread.reshape(row_count * BLOCK, col_count * BLOCK)


def dense_apply(left_operand, right_operand, kept_mask, product_kind):
    full_mask = expand_mask(kept_mask)
    if product_kind == "forward":
        masked = right_operand * full_mask.astype(right_operand.dtype)
        return jnp.dot(left_operand, masked, preferred_element_type=jnp.float32)
    if product_kind == "transposed":
        masked = right_operand * full_mask.astype(right_operand.dtype)
        return lax.dot_general(
            left_operand, masked, (((1,), (1,)), ((), ())), preferred_element_type=jnp.float32
        )
    product = lax.dot_general(
        left_operand, right_operand, (((0,), (0,)), ((), ())), preferred_element_type=jnp.float32
    )
    return product * full_mask.astype(jnp.float32)


def apply_blocks(left_operand, right_operand, kept_mask, product_kind):
    return dense_apply(left_operand, right_operand, kept_mask, product_kind)


def a2a_scatter_sum(parts, axis_name):
    count = lax.axis_size(axis_name)
    pieces = parts.reshape((count, parts.shape[0] // count) + parts.shape[1:])
    return lax.all_to_all(pieces, axis_name, 0, 0, tiled=True).sum(axis=0)


def a2a_gather(block, axis_name):
    count = lax.axis_size(axis_name)
    spread = jnp.broadcast_to(block[None], (count,) + block.shape)
    gathered = lax.all_to_all(spread, axis_name, 0, 0, tiled=True)
    return gathered.reshape((count * block.shape[0],) + block.shape[1:])


def on_device(tokens, cotangent, w_gate, w_up, w_down, order_gate, order_up, order_down):
    rows_here = w_gate.shape[0] // BLOCK
    cols_here = w_gate.shape[1] // BLOCK
    row_start = lax.axis_index("row") * rows_here
    col_start = lax.axis_index("col") * cols_here
    width_blocks = rows_here * lax.axis_size("row")
    hidden_blocks = cols_here * lax.axis_size("col")
    hidden_here = w_gate.shape[1]
    keep_gate = kept_table(order_gate, row_start, col_start, rows_here, cols_here, hidden_blocks)
    keep_up = kept_table(order_up, row_start, col_start, rows_here, cols_here, hidden_blocks)
    keep_down = kept_table(order_down, col_start, row_start, cols_here, rows_here, width_blocks)
    cotangent_all = lax.all_gather(cotangent, "col", axis=0, tiled=True)
    tokens_all = a2a_gather(tokens, "col")
    gate_term = apply_blocks(tokens_all, w_gate, keep_gate, "forward")
    up_term = apply_blocks(tokens_all, w_up, keep_up, "forward")
    both = a2a_scatter_sum(jnp.concatenate([gate_term, up_term], axis=1), "row")
    gate, up = both[:, :hidden_here], both[:, hidden_here:]
    hidden_term = apply_blocks(cotangent_all, w_down, keep_down, "transposed")
    hidden_grad = a2a_scatter_sum(hidden_term, "row")
    sigmoid_gate = jax.nn.sigmoid(gate)
    activation = gate * sigmoid_gate
    hidden = (activation * up).astype(jnp.bfloat16)
    hidden_all = a2a_gather(hidden, "row")
    output_term = apply_blocks(hidden_all, w_down, keep_down, "forward")
    output = lax.psum_scatter(output_term, "col", scatter_dimension=0, tiled=True).astype(
        jnp.bfloat16
    )
    gate_grad = (hidden_grad * up * sigmoid_gate * (1.0 + gate * (1.0 - sigmoid_gate))).astype(
        jnp.bfloat16
    )
    up_grad = (hidden_grad * activation).astype(jnp.bfloat16)
    grads_all = a2a_gather(jnp.concatenate([gate_grad, up_grad], axis=1), "row")
    gate_grad_all, up_grad_all = grads_all[:, :hidden_here], grads_all[:, hidden_here:]
    down_weight_grad = apply_blocks(hidden_all, cotangent_all, keep_down, "weights")
    gate_weight_grad = apply_blocks(tokens_all, gate_grad_all, keep_gate, "weights")
    up_weight_grad = apply_blocks(tokens_all, up_grad_all, keep_up, "weights")
    through_gate = apply_blocks(gate_grad_all, w_gate, keep_gate, "transposed")
    through_up = apply_blocks(up_grad_all, w_up, keep_up, "transposed")
    input_grad = a2a_scatter_sum(through_gate + through_up, "col")
    return (
        output,
        input_grad.astype(jnp.bfloat16),
        gate_weight_grad,
        up_weight_grad,
        down_weight_grad,
    )


def solution(mesh):
    placed = (
        P("col", "row"),
        P("col", "row"),
        P("row", "col"),
        P("row", "col"),
        P("col", "row"),
        P(),
        P(),
        P(),
    )
    return jax.shard_map(
        on_device,
        mesh=mesh,
        in_specs=placed,
        out_specs=(
            P("col", "row"),
            P("col", "row"),
            P("row", "col"),
            P("row", "col"),
            P("col", "row"),
        ),
        check_vma=False,
    )
```

```python
import jax
import jax.numpy as jnp
from jax import lax
from jax.sharding import PartitionSpec as P

BLOCK = 256


def kept_table(order, row_first, col_first, row_count, col_count, stride):
    kept_count = order.shape[0] // 2
    row_ids = row_first + jnp.arange(row_count, dtype=jnp.int32)
    col_ids = col_first + jnp.arange(col_count, dtype=jnp.int32)
    block_ids = row_ids[:, None] * stride + col_ids[None, :]
    return jnp.any(block_ids[:, :, None] == order[:kept_count][None, None, :], axis=2)


def expand_mask(kept_mask):
    row_count, col_count = kept_mask.shape
    spread = jnp.broadcast_to(kept_mask[:, None, :, None], (row_count, BLOCK, col_count, BLOCK))
    return spread.reshape(row_count * BLOCK, col_count * BLOCK)


def dense_apply(left_operand, right_operand, kept_mask, product_kind):
    full_mask = expand_mask(kept_mask)
    if product_kind == "forward":
        masked = right_operand * full_mask.astype(right_operand.dtype)
        return jnp.dot(left_operand, masked, preferred_element_type=jnp.float32)
    if product_kind == "transposed":
        masked = right_operand * full_mask.astype(right_operand.dtype)
        return lax.dot_general(
            left_operand, masked, (((1,), (1,)), ((), ())), preferred_element_type=jnp.float32
        )
    product = lax.dot_general(
        left_operand, right_operand, (((0,), (0,)), ((), ())), preferred_element_type=jnp.float32
    )
    return product * full_mask.astype(jnp.float32)


def apply_blocks(left_operand, right_operand, kept_mask, product_kind):
    return dense_apply(left_operand, right_operand, kept_mask, product_kind)


def a2a_scatter_sum(parts, axis_name):
    count = lax.axis_size(axis_name)
    pieces = parts.reshape((count, parts.shape[0] // count) + parts.shape[1:])
    return lax.all_to_all(pieces, axis_name, 0, 0, tiled=True).sum(axis=0)


def a2a_gather(block, axis_name):
    count = lax.axis_size(axis_name)
    spread = jnp.broadcast_to(block[None], (count,) + block.shape)
    gathered = lax.all_to_all(spread, axis_name, 0, 0, tiled=True)
    return gathered.reshape((count * block.shape[0],) + block.shape[1:])


def on_device(tokens, cotangent, w_gate, w_up, w_down, order_gate, order_up, order_down):
    rows_here = w_gate.shape[0] // BLOCK
    cols_here = w_gate.shape[1] // BLOCK
    row_start = lax.axis_index("row") * rows_here
    col_start = lax.axis_index("col") * cols_here
    width_blocks = rows_here * lax.axis_size("row")
    hidden_blocks = cols_here * lax.axis_size("col")
    hidden_here = w_gate.shape[1]
    keep_gate = kept_table(order_gate, row_start, col_start, rows_here, cols_here, hidden_blocks)
    keep_up = kept_table(order_up, row_start, col_start, rows_here, cols_here, hidden_blocks)
    keep_down = kept_table(order_down, col_start, row_start, cols_here, rows_here, width_blocks)
    width_here = tokens.shape[1]
    inputs_all = a2a_gather(jnp.concatenate([tokens, cotangent], axis=1), "col")
    tokens_all, cotangent_all = inputs_all[:, :width_here], inputs_all[:, width_here:]
    gate_term = apply_blocks(tokens_all, w_gate, keep_gate, "forward")
    up_term = apply_blocks(tokens_all, w_up, keep_up, "forward")
    hidden_term = apply_blocks(cotangent_all, w_down, keep_down, "transposed")
    sums = a2a_scatter_sum(jnp.concatenate([gate_term, up_term, hidden_term], axis=1), "row")
    gate = sums[:, :hidden_here]
    up = sums[:, hidden_here : 2 * hidden_here]
    hidden_grad = sums[:, 2 * hidden_here :]
    sigmoid_gate = jax.nn.sigmoid(gate)
    activation = gate * sigmoid_gate
    hidden = (activation * up).astype(jnp.bfloat16)
    gate_grad = (hidden_grad * up * sigmoid_gate * (1.0 + gate * (1.0 - sigmoid_gate))).astype(
        jnp.bfloat16
    )
    up_grad = (hidden_grad * activation).astype(jnp.bfloat16)
    acts_all = a2a_gather(jnp.concatenate([hidden, gate_grad, up_grad], axis=1), "row")
    hidden_all = acts_all[:, :hidden_here]
    gate_grad_all = acts_all[:, hidden_here : 2 * hidden_here]
    up_grad_all = acts_all[:, 2 * hidden_here :]
    output_term = apply_blocks(hidden_all, w_down, keep_down, "forward")
    down_weight_grad = apply_blocks(hidden_all, cotangent_all, keep_down, "weights")
    gate_weight_grad = apply_blocks(tokens_all, gate_grad_all, keep_gate, "weights")
    up_weight_grad = apply_blocks(tokens_all, up_grad_all, keep_up, "weights")
    through_gate = apply_blocks(gate_grad_all, w_gate, keep_gate, "transposed")
    through_up = apply_blocks(up_grad_all, w_up, keep_up, "transposed")
    outs = a2a_scatter_sum(jnp.concatenate([output_term, through_gate + through_up], axis=1), "col")
    output = outs[:, :width_here].astype(jnp.bfloat16)
    input_grad = outs[:, width_here:]
    return (
        output,
        input_grad.astype(jnp.bfloat16),
        gate_weight_grad,
        up_weight_grad,
        down_weight_grad,
    )


def solution(mesh):
    placed = (
        P("col", "row"),
        P("col", "row"),
        P("row", "col"),
        P("row", "col"),
        P("col", "row"),
        P(),
        P(),
        P(),
    )
    return jax.shard_map(
        on_device,
        mesh=mesh,
        in_specs=placed,
        out_specs=(
            P("col", "row"),
            P("col", "row"),
            P("row", "col"),
            P("row", "col"),
            P("col", "row"),
        ),
        check_vma=False,
    )
```

```python
import jax
import jax.numpy as jnp
from jax import lax
from jax.sharding import PartitionSpec as P

BLOCK = 256


def kept_table(order, row_first, col_first, row_count, col_count, stride):
    kept_count = order.shape[0] // 2
    row_ids = row_first + jnp.arange(row_count, dtype=jnp.int32)
    col_ids = col_first + jnp.arange(col_count, dtype=jnp.int32)
    block_ids = row_ids[:, None] * stride + col_ids[None, :]
    return jnp.any(block_ids[:, :, None] == order[:kept_count][None, None, :], axis=2)


def expand_mask(kept_mask):
    row_count, col_count = kept_mask.shape
    spread = jnp.broadcast_to(kept_mask[:, None, :, None], (row_count, BLOCK, col_count, BLOCK))
    return spread.reshape(row_count * BLOCK, col_count * BLOCK)


def dense_apply(left_operand, right_operand, kept_mask, product_kind):
    full_mask = expand_mask(kept_mask)
    if product_kind == "forward":
        masked = right_operand * full_mask.astype(right_operand.dtype)
        return jnp.dot(left_operand, masked, preferred_element_type=jnp.float32)
    if product_kind == "transposed":
        masked = right_operand * full_mask.astype(right_operand.dtype)
        return lax.dot_general(
            left_operand, masked, (((1,), (1,)), ((), ())), preferred_element_type=jnp.float32
        )
    product = lax.dot_general(
        left_operand, right_operand, (((0,), (0,)), ((), ())), preferred_element_type=jnp.float32
    )
    return product * full_mask.astype(jnp.float32)


def apply_blocks(left_operand, right_operand, kept_mask, product_kind):
    return dense_apply(left_operand, right_operand, kept_mask, product_kind)


def a2a_scatter_sum(parts, axis_name):
    count = lax.axis_size(axis_name)
    pieces = parts.reshape((count, parts.shape[0] // count) + parts.shape[1:])
    return lax.all_to_all(pieces, axis_name, 0, 0, tiled=True).sum(axis=0)


def a2a_gather(block, axis_name):
    count = lax.axis_size(axis_name)
    spread = jnp.broadcast_to(block[None], (count,) + block.shape)
    gathered = lax.all_to_all(spread, axis_name, 0, 0, tiled=True)
    return gathered.reshape((count * block.shape[0],) + block.shape[1:])


def ring_scatter_sum(parts, axis_name):
    count = lax.axis_size(axis_name)
    here = lax.axis_index(axis_name)
    pieces = parts.reshape((count, parts.shape[0] // count) + parts.shape[1:])
    half = parts.shape[1] // 2
    ahead, behind = pieces[:, :, :half], pieces[:, :, half:]
    forward = [(i, (i + 1) % count) for i in range(count)]
    backward = [(i, (i - 1) % count) for i in range(count)]
    carry_ahead = lax.dynamic_index_in_dim(ahead, (here - 1) % count, 0, keepdims=False)
    carry_behind = lax.dynamic_index_in_dim(behind, (here + 1) % count, 0, keepdims=False)
    for step in range(1, count):
        carry_ahead = lax.ppermute(carry_ahead, axis_name, forward) + lax.dynamic_index_in_dim(
            ahead, (here - 1 - step) % count, 0, keepdims=False
        )
        carry_behind = lax.ppermute(carry_behind, axis_name, backward) + lax.dynamic_index_in_dim(
            behind, (here + 1 + step) % count, 0, keepdims=False
        )
    return jnp.concatenate([carry_ahead, carry_behind], axis=1)


def on_device(tokens, cotangent, w_gate, w_up, w_down, order_gate, order_up, order_down):
    rows_here = w_gate.shape[0] // BLOCK
    cols_here = w_gate.shape[1] // BLOCK
    row_start = lax.axis_index("row") * rows_here
    col_start = lax.axis_index("col") * cols_here
    width_blocks = rows_here * lax.axis_size("row")
    hidden_blocks = cols_here * lax.axis_size("col")
    hidden_here = w_gate.shape[1]
    keep_gate = kept_table(order_gate, row_start, col_start, rows_here, cols_here, hidden_blocks)
    keep_up = kept_table(order_up, row_start, col_start, rows_here, cols_here, hidden_blocks)
    keep_down = kept_table(order_down, col_start, row_start, cols_here, rows_here, width_blocks)
    width_here = tokens.shape[1]
    inputs_all = a2a_gather(jnp.concatenate([tokens, cotangent], axis=1), "col")
    tokens_all, cotangent_all = inputs_all[:, :width_here], inputs_all[:, width_here:]
    gate_term = apply_blocks(tokens_all, w_gate, keep_gate, "forward")
    up_term = apply_blocks(tokens_all, w_up, keep_up, "forward")
    hidden_term = apply_blocks(cotangent_all, w_down, keep_down, "transposed")
    sums = ring_scatter_sum(jnp.concatenate([gate_term, up_term, hidden_term], axis=1), "row")
    gate = sums[:, :hidden_here]
    up = sums[:, hidden_here : 2 * hidden_here]
    hidden_grad = sums[:, 2 * hidden_here :]
    sigmoid_gate = jax.nn.sigmoid(gate)
    activation = gate * sigmoid_gate
    hidden = (activation * up).astype(jnp.bfloat16)
    gate_grad = (hidden_grad * up * sigmoid_gate * (1.0 + gate * (1.0 - sigmoid_gate))).astype(
        jnp.bfloat16
    )
    up_grad = (hidden_grad * activation).astype(jnp.bfloat16)
    acts_all = a2a_gather(jnp.concatenate([hidden, gate_grad, up_grad], axis=1), "row")
    hidden_all = acts_all[:, :hidden_here]
    gate_grad_all = acts_all[:, hidden_here : 2 * hidden_here]
    up_grad_all = acts_all[:, 2 * hidden_here :]
    output_term = apply_blocks(hidden_all, w_down, keep_down, "forward")
    down_weight_grad = apply_blocks(hidden_all, cotangent_all, keep_down, "weights")
    gate_weight_grad = apply_blocks(tokens_all, gate_grad_all, keep_gate, "weights")
    up_weight_grad = apply_blocks(tokens_all, up_grad_all, keep_up, "weights")
    through_gate = apply_blocks(gate_grad_all, w_gate, keep_gate, "transposed")
    through_up = apply_blocks(up_grad_all, w_up, keep_up, "transposed")
    outs = a2a_scatter_sum(jnp.concatenate([output_term, through_gate + through_up], axis=1), "col")
    output = outs[:, :width_here].astype(jnp.bfloat16)
    input_grad = outs[:, width_here:]
    return (
        output,
        input_grad.astype(jnp.bfloat16),
        gate_weight_grad,
        up_weight_grad,
        down_weight_grad,
    )


def solution(mesh):
    placed = (
        P("col", "row"),
        P("col", "row"),
        P("row", "col"),
        P("row", "col"),
        P("col", "row"),
        P(),
        P(),
        P(),
    )
    return jax.shard_map(
        on_device,
        mesh=mesh,
        in_specs=placed,
        out_specs=(
            P("col", "row"),
            P("col", "row"),
            P("row", "col"),
            P("row", "col"),
            P("col", "row"),
        ),
        check_vma=False,
    )
```

```python
import jax
import jax.numpy as jnp
from jax import lax
from jax.sharding import Mesh, PartitionSpec as P

BLOCK = 256


def kept_table(order, row_first, col_first, row_count, col_count, stride):
    kept_count = order.shape[0] // 2
    row_ids = row_first + jnp.arange(row_count, dtype=jnp.int32)
    col_ids = col_first + jnp.arange(col_count, dtype=jnp.int32)
    block_ids = row_ids[:, None] * stride + col_ids[None, :]
    return jnp.any(block_ids[:, :, None] == order[:kept_count][None, None, :], axis=2)


def expand_mask(kept_mask):
    row_count, col_count = kept_mask.shape
    spread = jnp.broadcast_to(kept_mask[:, None, :, None], (row_count, BLOCK, col_count, BLOCK))
    return spread.reshape(row_count * BLOCK, col_count * BLOCK)


def dense_apply(left_operand, right_operand, kept_mask, product_kind):
    full_mask = expand_mask(kept_mask)
    if product_kind == "forward":
        masked = right_operand * full_mask.astype(right_operand.dtype)
        return jnp.dot(left_operand, masked, preferred_element_type=jnp.float32)
    if product_kind == "transposed":
        masked = right_operand * full_mask.astype(right_operand.dtype)
        return lax.dot_general(
            left_operand, masked, (((1,), (1,)), ((), ())), preferred_element_type=jnp.float32
        )
    product = lax.dot_general(
        left_operand, right_operand, (((0,), (0,)), ((), ())), preferred_element_type=jnp.float32
    )
    return product * full_mask.astype(jnp.float32)


def apply_blocks(left_operand, right_operand, kept_mask, product_kind):
    return dense_apply(left_operand, right_operand, kept_mask, product_kind)


def a2a_scatter_sum(parts, axis_name):
    count = lax.axis_size(axis_name)
    pieces = parts.reshape((count, parts.shape[0] // count) + parts.shape[1:])
    return lax.all_to_all(pieces, axis_name, 0, 0, tiled=True).sum(axis=0)


def a2a_gather(block, axis_name):
    count = lax.axis_size(axis_name)
    spread = jnp.broadcast_to(block[None], (count,) + block.shape)
    gathered = lax.all_to_all(spread, axis_name, 0, 0, tiled=True)
    return gathered.reshape((count * block.shape[0],) + block.shape[1:])


def ring_scatter_sum(parts, axis_name):
    count = lax.axis_size(axis_name)
    here = lax.axis_index(axis_name)
    pieces = parts.reshape((count, parts.shape[0] // count) + parts.shape[1:])
    half = parts.shape[1] // 2
    ahead, behind = pieces[:, :, :half], pieces[:, :, half:]
    forward = [(i, (i + 1) % count) for i in range(count)]
    backward = [(i, (i - 1) % count) for i in range(count)]
    carry_ahead = lax.dynamic_index_in_dim(ahead, (here - 1) % count, 0, keepdims=False)
    carry_behind = lax.dynamic_index_in_dim(behind, (here + 1) % count, 0, keepdims=False)
    for step in range(1, count):
        carry_ahead = lax.ppermute(carry_ahead, axis_name, forward) + lax.dynamic_index_in_dim(
            ahead, (here - 1 - step) % count, 0, keepdims=False
        )
        carry_behind = lax.ppermute(carry_behind, axis_name, backward) + lax.dynamic_index_in_dim(
            behind, (here + 1 + step) % count, 0, keepdims=False
        )
    return jnp.concatenate([carry_ahead, carry_behind], axis=1)


def col_gather(block):
    chips = lax.axis_size("chip")
    core = lax.axis_index("core")
    spread = jnp.broadcast_to(block[None], (chips,) + block.shape)
    mine = lax.all_to_all(spread, "chip", 0, 0, tiled=True)
    other = lax.ppermute(mine, "core", [(0, 1), (1, 0)])
    paired = jnp.where(core == 0, jnp.stack([mine, other], 1), jnp.stack([other, mine], 1))
    return paired.reshape((chips * 2 * block.shape[0],) + block.shape[1:])


def col_scatter_sum(parts):
    chips = lax.axis_size("chip")
    core = lax.axis_index("core")
    pieces = parts.reshape((chips, 2, parts.shape[0] // (2 * chips)) + parts.shape[1:])
    mine = lax.dynamic_index_in_dim(pieces, core, 1, keepdims=False)
    other = lax.dynamic_index_in_dim(pieces, 1 - core, 1, keepdims=False)
    pair_sum = mine + lax.ppermute(other, "core", [(0, 1), (1, 0)])
    return lax.all_to_all(pair_sum, "chip", 0, 0, tiled=True).sum(axis=0)


def on_device(tokens, cotangent, w_gate, w_up, w_down, order_gate, order_up, order_down):
    rows_here = w_gate.shape[0] // BLOCK
    cols_here = w_gate.shape[1] // BLOCK
    row_start = lax.axis_index("row") * rows_here
    col_start = (lax.axis_index("chip") * 2 + lax.axis_index("core")) * cols_here
    width_blocks = rows_here * lax.axis_size("row")
    hidden_blocks = cols_here * lax.axis_size("chip") * 2
    hidden_here = w_gate.shape[1]
    keep_gate = kept_table(order_gate, row_start, col_start, rows_here, cols_here, hidden_blocks)
    keep_up = kept_table(order_up, row_start, col_start, rows_here, cols_here, hidden_blocks)
    keep_down = kept_table(order_down, col_start, row_start, cols_here, rows_here, width_blocks)
    width_here = tokens.shape[1]
    inputs_all = col_gather(jnp.concatenate([tokens, cotangent], axis=1))
    tokens_all, cotangent_all = inputs_all[:, :width_here], inputs_all[:, width_here:]
    gate_term = apply_blocks(tokens_all, w_gate, keep_gate, "forward")
    up_term = apply_blocks(tokens_all, w_up, keep_up, "forward")
    hidden_term = apply_blocks(cotangent_all, w_down, keep_down, "transposed")
    sums = ring_scatter_sum(jnp.concatenate([gate_term, up_term, hidden_term], axis=1), "row")
    gate = sums[:, :hidden_here]
    up = sums[:, hidden_here : 2 * hidden_here]
    hidden_grad = sums[:, 2 * hidden_here :]
    sigmoid_gate = jax.nn.sigmoid(gate)
    activation = gate * sigmoid_gate
    hidden = (activation * up).astype(jnp.bfloat16)
    gate_grad = (hidden_grad * up * sigmoid_gate * (1.0 + gate * (1.0 - sigmoid_gate))).astype(
        jnp.bfloat16
    )
    up_grad = (hidden_grad * activation).astype(jnp.bfloat16)
    acts_all = a2a_gather(jnp.concatenate([hidden, gate_grad, up_grad], axis=1), "row")
    hidden_all = acts_all[:, :hidden_here]
    gate_grad_all = acts_all[:, hidden_here : 2 * hidden_here]
    up_grad_all = acts_all[:, 2 * hidden_here :]
    output_term = apply_blocks(hidden_all, w_down, keep_down, "forward")
    down_weight_grad = apply_blocks(hidden_all, cotangent_all, keep_down, "weights")
    gate_weight_grad = apply_blocks(tokens_all, gate_grad_all, keep_gate, "weights")
    up_weight_grad = apply_blocks(tokens_all, up_grad_all, keep_up, "weights")
    through_gate = apply_blocks(gate_grad_all, w_gate, keep_gate, "transposed")
    through_up = apply_blocks(up_grad_all, w_up, keep_up, "transposed")
    outs = col_scatter_sum(jnp.concatenate([output_term, through_gate + through_up], axis=1))
    output = outs[:, :width_here].astype(jnp.bfloat16)
    input_grad = outs[:, width_here:]
    return (
        output,
        input_grad.astype(jnp.bfloat16),
        gate_weight_grad,
        up_weight_grad,
        down_weight_grad,
    )


def solution(mesh):
    rows, cols = mesh.devices.shape
    split = Mesh(mesh.devices.reshape(rows, cols // 2, 2), ("row", "chip", "core"))
    col = ("chip", "core")
    placed = (
        P(col, "row"),
        P(col, "row"),
        P("row", col),
        P("row", col),
        P(col, "row"),
        P(),
        P(),
        P(),
    )
    return jax.shard_map(
        on_device,
        mesh=split,
        in_specs=placed,
        out_specs=(
            P(col, "row"),
            P(col, "row"),
            P("row", col),
            P("row", col),
            P(col, "row"),
        ),
        check_vma=False,
    )
```

```python
import jax
import jax.numpy as jnp
from jax import lax
from jax.sharding import Mesh, PartitionSpec as P

BLOCK = 256


def kept_table(order, row_first, col_first, row_count, col_count, stride):
    kept_count = order.shape[0] // 2
    row_ids = row_first + jnp.arange(row_count, dtype=jnp.int32)
    col_ids = col_first + jnp.arange(col_count, dtype=jnp.int32)
    block_ids = row_ids[:, None] * stride + col_ids[None, :]
    return jnp.any(block_ids[:, :, None] == order[:kept_count][None, None, :], axis=2)


def expand_mask(kept_mask):
    row_count, col_count = kept_mask.shape
    spread = jnp.broadcast_to(kept_mask[:, None, :, None], (row_count, BLOCK, col_count, BLOCK))
    return spread.reshape(row_count * BLOCK, col_count * BLOCK)


def dense_apply(left_operand, right_operand, kept_mask, product_kind):
    full_mask = expand_mask(kept_mask)
    if product_kind == "forward":
        masked = right_operand * full_mask.astype(right_operand.dtype)
        return jnp.dot(left_operand, masked, preferred_element_type=jnp.float32)
    if product_kind == "transposed":
        masked = right_operand * full_mask.astype(right_operand.dtype)
        return lax.dot_general(
            left_operand, masked, (((1,), (1,)), ((), ())), preferred_element_type=jnp.float32
        )
    product = lax.dot_general(
        left_operand, right_operand, (((0,), (0,)), ((), ())), preferred_element_type=jnp.float32
    )
    return product * full_mask.astype(jnp.float32)


def apply_blocks(left_operand, right_operand, kept_mask, product_kind):
    return dense_apply(left_operand, right_operand, kept_mask, product_kind)


def a2a_scatter_sum(parts, axis_name):
    count = lax.axis_size(axis_name)
    pieces = parts.reshape((count, parts.shape[0] // count) + parts.shape[1:])
    return lax.all_to_all(pieces, axis_name, 0, 0, tiled=True).sum(axis=0)


def a2a_gather(block, axis_name):
    count = lax.axis_size(axis_name)
    spread = jnp.broadcast_to(block[None], (count,) + block.shape)
    gathered = lax.all_to_all(spread, axis_name, 0, 0, tiled=True)
    return gathered.reshape((count * block.shape[0],) + block.shape[1:])


def ring_scatter_sum(parts, axis_name):
    count = lax.axis_size(axis_name)
    here = lax.axis_index(axis_name)
    pieces = parts.reshape((count, parts.shape[0] // count) + parts.shape[1:])
    half = parts.shape[1] // 2
    ahead, behind = pieces[:, :, :half], pieces[:, :, half:]
    forward = [(i, (i + 1) % count) for i in range(count)]
    backward = [(i, (i - 1) % count) for i in range(count)]
    carry_ahead = lax.dynamic_index_in_dim(ahead, (here - 1) % count, 0, keepdims=False)
    carry_behind = lax.dynamic_index_in_dim(behind, (here + 1) % count, 0, keepdims=False)
    for step in range(1, count):
        carry_ahead = lax.ppermute(carry_ahead, axis_name, forward) + lax.dynamic_index_in_dim(
            ahead, (here - 1 - step) % count, 0, keepdims=False
        )
        carry_behind = lax.ppermute(carry_behind, axis_name, backward) + lax.dynamic_index_in_dim(
            behind, (here + 1 + step) % count, 0, keepdims=False
        )
    return jnp.concatenate([carry_ahead, carry_behind], axis=1)


def relay_scatter_sum(parts, axis_name):
    count = lax.axis_size(axis_name)
    here = lax.axis_index(axis_name)
    pieces = parts.reshape((count, parts.shape[0] // count) + parts.shape[1:])

    def piece_for(offset):
        return lax.dynamic_index_in_dim(pieces, (here + offset) % count, 0, keepdims=False)

    forward = [(i, (i + 1) % count) for i in range(count)]
    backward = [(i, (i - 1) % count) for i in range(count)]
    ahead = count // 2
    behind = count - 1 - ahead
    carry_ahead = piece_for(ahead)
    carry_behind = piece_for(-behind)
    for step in range(1, ahead + 1):
        carry_ahead = lax.ppermute(carry_ahead, axis_name, forward)
        if step < ahead:
            carry_ahead = carry_ahead + piece_for(ahead - step)
        if step <= behind:
            carry_behind = lax.ppermute(carry_behind, axis_name, backward)
            if step < behind:
                carry_behind = carry_behind + piece_for(step - behind)
    return piece_for(0) + carry_ahead + carry_behind


def relay_gather(block, axis_name):
    count = lax.axis_size(axis_name)
    here = lax.axis_index(axis_name)
    forward = [(i, (i + 1) % count) for i in range(count)]
    backward = [(i, (i - 1) % count) for i in range(count)]
    ahead = count // 2
    behind = count - 1 - ahead
    from_behind, from_ahead = [], []
    carry_ahead, carry_behind = block, block
    for step in range(1, ahead + 1):
        carry_ahead = lax.ppermute(carry_ahead, axis_name, forward)
        from_behind.append(carry_ahead)
        if step <= behind:
            carry_behind = lax.ppermute(carry_behind, axis_name, backward)
            from_ahead.append(carry_behind)
    by_offset = jnp.stack([block] + from_ahead + from_behind[::-1])
    placed = jnp.roll(by_offset, here, axis=0)
    return placed.reshape((count * block.shape[0],) + block.shape[1:])


def col_gather(block):
    chips = lax.axis_size("chip")
    core = lax.axis_index("core")
    spread = jnp.broadcast_to(block[None], (chips,) + block.shape)
    mine = lax.all_to_all(spread, "chip", 0, 0, tiled=True)
    other = lax.ppermute(mine, "core", [(0, 1), (1, 0)])
    paired = jnp.where(core == 0, jnp.stack([mine, other], 1), jnp.stack([other, mine], 1))
    return paired.reshape((chips * 2 * block.shape[0],) + block.shape[1:])


def col_scatter_sum(parts):
    chips = lax.axis_size("chip")
    core = lax.axis_index("core")
    pieces = parts.reshape((chips, 2, parts.shape[0] // (2 * chips)) + parts.shape[1:])
    mine = lax.dynamic_index_in_dim(pieces, core, 1, keepdims=False)
    other = lax.dynamic_index_in_dim(pieces, 1 - core, 1, keepdims=False)
    pair_sum = mine + lax.ppermute(other, "core", [(0, 1), (1, 0)])
    return lax.all_to_all(pair_sum, "chip", 0, 0, tiled=True).sum(axis=0)


def on_device(tokens, cotangent, w_gate, w_up, w_down, order_gate, order_up, order_down):
    rows_here = w_gate.shape[0] // BLOCK
    cols_here = w_gate.shape[1] // BLOCK
    row_start = lax.axis_index("row") * rows_here
    col_start = (lax.axis_index("chip") * 2 + lax.axis_index("core")) * cols_here
    width_blocks = rows_here * lax.axis_size("row")
    hidden_blocks = cols_here * lax.axis_size("chip") * 2
    hidden_here = w_gate.shape[1]
    keep_gate = kept_table(order_gate, row_start, col_start, rows_here, cols_here, hidden_blocks)
    keep_up = kept_table(order_up, row_start, col_start, rows_here, cols_here, hidden_blocks)
    keep_down = kept_table(order_down, col_start, row_start, cols_here, rows_here, width_blocks)
    width_here = tokens.shape[1]
    inputs_all = col_gather(jnp.concatenate([tokens, cotangent], axis=1))
    tokens_all, cotangent_all = inputs_all[:, :width_here], inputs_all[:, width_here:]
    gate_term = apply_blocks(tokens_all, w_gate, keep_gate, "forward")
    up_term = apply_blocks(tokens_all, w_up, keep_up, "forward")
    hidden_term = apply_blocks(cotangent_all, w_down, keep_down, "transposed")
    sums = relay_scatter_sum(jnp.concatenate([gate_term, up_term, hidden_term], axis=1), "row")
    gate = sums[:, :hidden_here]
    up = sums[:, hidden_here : 2 * hidden_here]
    hidden_grad = sums[:, 2 * hidden_here :]
    sigmoid_gate = jax.nn.sigmoid(gate)
    activation = gate * sigmoid_gate
    hidden = (activation * up).astype(jnp.bfloat16)
    gate_grad = (hidden_grad * up * sigmoid_gate * (1.0 + gate * (1.0 - sigmoid_gate))).astype(
        jnp.bfloat16
    )
    up_grad = (hidden_grad * activation).astype(jnp.bfloat16)
    acts_all = relay_gather(jnp.concatenate([hidden, gate_grad, up_grad], axis=1), "row")
    hidden_all = acts_all[:, :hidden_here]
    gate_grad_all = acts_all[:, hidden_here : 2 * hidden_here]
    up_grad_all = acts_all[:, 2 * hidden_here :]
    output_term = apply_blocks(hidden_all, w_down, keep_down, "forward")
    down_weight_grad = apply_blocks(hidden_all, cotangent_all, keep_down, "weights")
    gate_weight_grad = apply_blocks(tokens_all, gate_grad_all, keep_gate, "weights")
    up_weight_grad = apply_blocks(tokens_all, up_grad_all, keep_up, "weights")
    through_gate = apply_blocks(gate_grad_all, w_gate, keep_gate, "transposed")
    through_up = apply_blocks(up_grad_all, w_up, keep_up, "transposed")
    outs = col_scatter_sum(jnp.concatenate([output_term, through_gate + through_up], axis=1))
    output = outs[:, :width_here].astype(jnp.bfloat16)
    input_grad = outs[:, width_here:]
    return (
        output,
        input_grad.astype(jnp.bfloat16),
        gate_weight_grad,
        up_weight_grad,
        down_weight_grad,
    )


def solution(mesh):
    rows, cols = mesh.devices.shape
    split = Mesh(mesh.devices.reshape(rows, cols // 2, 2), ("row", "chip", "core"))
    col = ("chip", "core")
    placed = (
        P(col, "row"),
        P(col, "row"),
        P("row", col),
        P("row", col),
        P(col, "row"),
        P(),
        P(),
        P(),
    )
    return jax.shard_map(
        on_device,
        mesh=split,
        in_specs=placed,
        out_specs=(
            P(col, "row"),
            P(col, "row"),
            P("row", col),
            P("row", col),
            P(col, "row"),
        ),
        check_vma=False,
    )
```

```python
import jax
import jax.numpy as jnp
from jax import lax
from jax.sharding import Mesh, PartitionSpec as P

BLOCK = 256


def kept_table(order, row_first, col_first, row_count, col_count, stride):
    kept_count = order.shape[0] // 2
    row_ids = row_first + jnp.arange(row_count, dtype=jnp.int32)
    col_ids = col_first + jnp.arange(col_count, dtype=jnp.int32)
    block_ids = row_ids[:, None] * stride + col_ids[None, :]
    return jnp.any(block_ids[:, :, None] == order[:kept_count][None, None, :], axis=2)


def expand_mask(kept_mask):
    row_count, col_count = kept_mask.shape
    spread = jnp.broadcast_to(kept_mask[:, None, :, None], (row_count, BLOCK, col_count, BLOCK))
    return spread.reshape(row_count * BLOCK, col_count * BLOCK)


def dense_apply(left_operand, right_operand, kept_mask, product_kind):
    full_mask = expand_mask(kept_mask)
    if product_kind == "forward":
        masked = right_operand * full_mask.astype(right_operand.dtype)
        return jnp.dot(left_operand, masked, preferred_element_type=jnp.float32)
    if product_kind == "transposed":
        masked = right_operand * full_mask.astype(right_operand.dtype)
        return lax.dot_general(
            left_operand, masked, (((1,), (1,)), ((), ())), preferred_element_type=jnp.float32
        )
    product = lax.dot_general(
        left_operand, right_operand, (((0,), (0,)), ((), ())), preferred_element_type=jnp.float32
    )
    return product * full_mask.astype(jnp.float32)


def apply_blocks(left_operand, right_operand, kept_mask, product_kind):
    return dense_apply(left_operand, right_operand, kept_mask, product_kind)


def a2a_scatter_sum(parts, axis_name):
    count = lax.axis_size(axis_name)
    pieces = parts.reshape((count, parts.shape[0] // count) + parts.shape[1:])
    return lax.all_to_all(pieces, axis_name, 0, 0, tiled=True).sum(axis=0)


def a2a_gather(block, axis_name):
    count = lax.axis_size(axis_name)
    spread = jnp.broadcast_to(block[None], (count,) + block.shape)
    gathered = lax.all_to_all(spread, axis_name, 0, 0, tiled=True)
    return gathered.reshape((count * block.shape[0],) + block.shape[1:])


def ring_scatter_sum(parts, axis_name):
    count = lax.axis_size(axis_name)
    here = lax.axis_index(axis_name)
    pieces = parts.reshape((count, parts.shape[0] // count) + parts.shape[1:])
    half = parts.shape[1] // 2
    ahead, behind = pieces[:, :, :half], pieces[:, :, half:]
    forward = [(i, (i + 1) % count) for i in range(count)]
    backward = [(i, (i - 1) % count) for i in range(count)]
    carry_ahead = lax.dynamic_index_in_dim(ahead, (here - 1) % count, 0, keepdims=False)
    carry_behind = lax.dynamic_index_in_dim(behind, (here + 1) % count, 0, keepdims=False)
    for step in range(1, count):
        carry_ahead = lax.ppermute(carry_ahead, axis_name, forward) + lax.dynamic_index_in_dim(
            ahead, (here - 1 - step) % count, 0, keepdims=False
        )
        carry_behind = lax.ppermute(carry_behind, axis_name, backward) + lax.dynamic_index_in_dim(
            behind, (here + 1 + step) % count, 0, keepdims=False
        )
    return jnp.concatenate([carry_ahead, carry_behind], axis=1)


def relay_scatter_sum(parts, axis_name):
    count = lax.axis_size(axis_name)
    here = lax.axis_index(axis_name)
    pieces = parts.reshape((count, parts.shape[0] // count) + parts.shape[1:])
    half = parts.shape[1] // 2
    spans = (slice(0, half), slice(half, parts.shape[1]))

    def piece_for(offset, span):
        return lax.dynamic_index_in_dim(pieces, (here + offset) % count, 0, keepdims=False)[:, span]

    forward = [(i, (i + 1) % count) for i in range(count)]
    backward = [(i, (i - 1) % count) for i in range(count)]
    longer = count // 2
    shorter = count - 1 - longer
    reach = ((longer, shorter), (shorter, longer))
    ahead = [piece_for(r[0], span) for r, span in zip(reach, spans)]
    behind = [piece_for(-r[1], span) for r, span in zip(reach, spans)]
    for step in range(1, longer + 1):
        going = [c for c, r in enumerate(reach) if step <= r[0]]
        coming = [c for c, r in enumerate(reach) if step <= r[1]]
        sent_ahead = lax.ppermute(tuple(ahead[c] for c in going), axis_name, forward)
        sent_behind = lax.ppermute(tuple(behind[c] for c in coming), axis_name, backward)
        for c, value in zip(going, sent_ahead):
            ahead[c] = value + piece_for(reach[c][0] - step, spans[c]) if step < reach[c][0] else value
        for c, value in zip(coming, sent_behind):
            behind[c] = value + piece_for(step - reach[c][1], spans[c]) if step < reach[c][1] else value
    return jnp.concatenate(
        [piece_for(0, span) + ahead[c] + behind[c] for c, span in enumerate(spans)], axis=1
    )


def relay_gather(block, axis_name):
    count = lax.axis_size(axis_name)
    here = lax.axis_index(axis_name)
    forward = [(i, (i + 1) % count) for i in range(count)]
    backward = [(i, (i - 1) % count) for i in range(count)]
    ahead = count // 2
    behind = count - 1 - ahead
    from_behind, from_ahead = [], []
    carry_ahead, carry_behind = block, block
    for step in range(1, ahead + 1):
        carry_ahead = lax.ppermute(carry_ahead, axis_name, forward)
        from_behind.append(carry_ahead)
        if step <= behind:
            carry_behind = lax.ppermute(carry_behind, axis_name, backward)
            from_ahead.append(carry_behind)
    by_offset = jnp.stack([block] + from_ahead + from_behind[::-1])
    placed = jnp.roll(by_offset, here, axis=0)
    return placed.reshape((count * block.shape[0],) + block.shape[1:])


def col_gather(block):
    chips = lax.axis_size("chip")
    core = lax.axis_index("core")
    spread = jnp.broadcast_to(block[None], (chips,) + block.shape)
    mine = lax.all_to_all(spread, "chip", 0, 0, tiled=True)
    other = lax.ppermute(mine, "core", [(0, 1), (1, 0)])
    paired = jnp.where(core == 0, jnp.stack([mine, other], 1), jnp.stack([other, mine], 1))
    return paired.reshape((chips * 2 * block.shape[0],) + block.shape[1:])


def col_scatter_sum(parts):
    chips = lax.axis_size("chip")
    core = lax.axis_index("core")
    pieces = parts.reshape((chips, 2, parts.shape[0] // (2 * chips)) + parts.shape[1:])
    mine = lax.dynamic_index_in_dim(pieces, core, 1, keepdims=False)
    other = lax.dynamic_index_in_dim(pieces, 1 - core, 1, keepdims=False)
    pair_sum = mine + lax.ppermute(other, "core", [(0, 1), (1, 0)])
    return lax.all_to_all(pair_sum, "chip", 0, 0, tiled=True).sum(axis=0)


def on_device(tokens, cotangent, w_gate, w_up, w_down, order_gate, order_up, order_down):
    rows_here = w_gate.shape[0] // BLOCK
    cols_here = w_gate.shape[1] // BLOCK
    row_start = lax.axis_index("row") * rows_here
    col_start = (lax.axis_index("chip") * 2 + lax.axis_index("core")) * cols_here
    width_blocks = rows_here * lax.axis_size("row")
    hidden_blocks = cols_here * lax.axis_size("chip") * 2
    hidden_here = w_gate.shape[1]
    keep_gate = kept_table(order_gate, row_start, col_start, rows_here, cols_here, hidden_blocks)
    keep_up = kept_table(order_up, row_start, col_start, rows_here, cols_here, hidden_blocks)
    keep_down = kept_table(order_down, col_start, row_start, cols_here, rows_here, width_blocks)
    width_here = tokens.shape[1]
    inputs_all = col_gather(jnp.concatenate([tokens, cotangent], axis=1))
    tokens_all, cotangent_all = inputs_all[:, :width_here], inputs_all[:, width_here:]
    gate_term = apply_blocks(tokens_all, w_gate, keep_gate, "forward")
    up_term = apply_blocks(tokens_all, w_up, keep_up, "forward")
    hidden_term = apply_blocks(cotangent_all, w_down, keep_down, "transposed")
    sums = relay_scatter_sum(jnp.concatenate([gate_term, up_term, hidden_term], axis=1), "row")
    gate = sums[:, :hidden_here]
    up = sums[:, hidden_here : 2 * hidden_here]
    hidden_grad = sums[:, 2 * hidden_here :]
    sigmoid_gate = jax.nn.sigmoid(gate)
    activation = gate * sigmoid_gate
    hidden = (activation * up).astype(jnp.bfloat16)
    gate_grad = (hidden_grad * up * sigmoid_gate * (1.0 + gate * (1.0 - sigmoid_gate))).astype(
        jnp.bfloat16
    )
    up_grad = (hidden_grad * activation).astype(jnp.bfloat16)
    acts_all = relay_gather(jnp.concatenate([hidden, gate_grad, up_grad], axis=1), "row")
    hidden_all = acts_all[:, :hidden_here]
    gate_grad_all = acts_all[:, hidden_here : 2 * hidden_here]
    up_grad_all = acts_all[:, 2 * hidden_here :]
    output_term = apply_blocks(hidden_all, w_down, keep_down, "forward")
    down_weight_grad = apply_blocks(hidden_all, cotangent_all, keep_down, "weights")
    gate_weight_grad = apply_blocks(tokens_all, gate_grad_all, keep_gate, "weights")
    up_weight_grad = apply_blocks(tokens_all, up_grad_all, keep_up, "weights")
    through_gate = apply_blocks(gate_grad_all, w_gate, keep_gate, "transposed")
    through_up = apply_blocks(up_grad_all, w_up, keep_up, "transposed")
    outs = col_scatter_sum(jnp.concatenate([output_term, through_gate + through_up], axis=1))
    output = outs[:, :width_here].astype(jnp.bfloat16)
    input_grad = outs[:, width_here:]
    return (
        output,
        input_grad.astype(jnp.bfloat16),
        gate_weight_grad,
        up_weight_grad,
        down_weight_grad,
    )


def solution(mesh):
    rows, cols = mesh.devices.shape
    split = Mesh(mesh.devices.reshape(rows, cols // 2, 2), ("row", "chip", "core"))
    col = ("chip", "core")
    placed = (
        P(col, "row"),
        P(col, "row"),
        P("row", col),
        P("row", col),
        P(col, "row"),
        P(),
        P(),
        P(),
    )
    return jax.shard_map(
        on_device,
        mesh=split,
        in_specs=placed,
        out_specs=(
            P(col, "row"),
            P(col, "row"),
            P("row", col),
            P("row", col),
            P(col, "row"),
        ),
        check_vma=False,
    )
```

```python
import jax
import jax.numpy as jnp
from jax import lax
from jax.sharding import Mesh, PartitionSpec as P

BLOCK = 256


def kept_table(order, row_first, col_first, row_count, col_count, stride):
    kept_count = order.shape[0] // 2
    row_ids = row_first + jnp.arange(row_count, dtype=jnp.int32)
    col_ids = col_first + jnp.arange(col_count, dtype=jnp.int32)
    block_ids = row_ids[:, None] * stride + col_ids[None, :]
    return jnp.any(block_ids[:, :, None] == order[:kept_count][None, None, :], axis=2)


def expand_mask(kept_mask):
    row_count, col_count = kept_mask.shape
    spread = jnp.broadcast_to(kept_mask[:, None, :, None], (row_count, BLOCK, col_count, BLOCK))
    return spread.reshape(row_count * BLOCK, col_count * BLOCK)


def dense_apply(left_operand, right_operand, kept_mask, product_kind):
    full_mask = expand_mask(kept_mask)
    if product_kind == "forward":
        masked = right_operand * full_mask.astype(right_operand.dtype)
        return jnp.dot(left_operand, masked, preferred_element_type=jnp.float32)
    if product_kind == "transposed":
        masked = right_operand * full_mask.astype(right_operand.dtype)
        return lax.dot_general(
            left_operand, masked, (((1,), (1,)), ((), ())), preferred_element_type=jnp.float32
        )
    product = lax.dot_general(
        left_operand, right_operand, (((0,), (0,)), ((), ())), preferred_element_type=jnp.float32
    )
    return product * full_mask.astype(jnp.float32)


def apply_blocks(left_operand, right_operand, kept_mask, product_kind):
    return dense_apply(left_operand, right_operand, kept_mask, product_kind)


def a2a_scatter_sum(parts, axis_name):
    count = lax.axis_size(axis_name)
    pieces = parts.reshape((count, parts.shape[0] // count) + parts.shape[1:])
    return lax.all_to_all(pieces, axis_name, 0, 0, tiled=True).sum(axis=0)


def a2a_gather(block, axis_name):
    count = lax.axis_size(axis_name)
    spread = jnp.broadcast_to(block[None], (count,) + block.shape)
    gathered = lax.all_to_all(spread, axis_name, 0, 0, tiled=True)
    return gathered.reshape((count * block.shape[0],) + block.shape[1:])


def ring_scatter_sum(parts, axis_name):
    count = lax.axis_size(axis_name)
    here = lax.axis_index(axis_name)
    pieces = parts.reshape((count, parts.shape[0] // count) + parts.shape[1:])
    half = parts.shape[1] // 2
    ahead, behind = pieces[:, :, :half], pieces[:, :, half:]
    forward = [(i, (i + 1) % count) for i in range(count)]
    backward = [(i, (i - 1) % count) for i in range(count)]
    carry_ahead = lax.dynamic_index_in_dim(ahead, (here - 1) % count, 0, keepdims=False)
    carry_behind = lax.dynamic_index_in_dim(behind, (here + 1) % count, 0, keepdims=False)
    for step in range(1, count):
        carry_ahead = lax.ppermute(carry_ahead, axis_name, forward) + lax.dynamic_index_in_dim(
            ahead, (here - 1 - step) % count, 0, keepdims=False
        )
        carry_behind = lax.ppermute(carry_behind, axis_name, backward) + lax.dynamic_index_in_dim(
            behind, (here + 1 + step) % count, 0, keepdims=False
        )
    return jnp.concatenate([carry_ahead, carry_behind], axis=1)


def joint_permute(values, axis_name, pairs):
    if len(values) == 1:
        return [lax.ppermute(values[0], axis_name, pairs)]
    widths = [v.shape[1] for v in values]
    moved = lax.ppermute(jnp.concatenate(values, axis=1), axis_name, pairs)
    edges = [sum(widths[:k]) for k in range(len(widths) + 1)]
    return [moved[:, edges[k] : edges[k + 1]] for k in range(len(values))]


def relay_scatter_sum(parts, axis_name):
    count = lax.axis_size(axis_name)
    here = lax.axis_index(axis_name)
    pieces = parts.reshape((count, parts.shape[0] // count) + parts.shape[1:])
    half = parts.shape[1] // 2
    spans = (slice(0, half), slice(half, parts.shape[1]))

    def piece_for(offset, span):
        return lax.dynamic_index_in_dim(pieces, (here + offset) % count, 0, keepdims=False)[:, span]

    forward = [(i, (i + 1) % count) for i in range(count)]
    backward = [(i, (i - 1) % count) for i in range(count)]
    longer = count // 2
    shorter = count - 1 - longer
    reach = ((longer, shorter), (shorter, longer))
    ahead = [piece_for(r[0], span) for r, span in zip(reach, spans)]
    behind = [piece_for(-r[1], span) for r, span in zip(reach, spans)]
    for step in range(1, longer + 1):
        going = [c for c, r in enumerate(reach) if step <= r[0]]
        coming = [c for c, r in enumerate(reach) if step <= r[1]]
        sent_ahead = joint_permute([ahead[c] for c in going], axis_name, forward)
        sent_behind = joint_permute([behind[c] for c in coming], axis_name, backward)
        for c, value in zip(going, sent_ahead):
            ahead[c] = value + piece_for(reach[c][0] - step, spans[c]) if step < reach[c][0] else value
        for c, value in zip(coming, sent_behind):
            behind[c] = value + piece_for(step - reach[c][1], spans[c]) if step < reach[c][1] else value
    return jnp.concatenate(
        [piece_for(0, span) + ahead[c] + behind[c] for c, span in enumerate(spans)], axis=1
    )


def relay_gather(block, axis_name):
    count = lax.axis_size(axis_name)
    here = lax.axis_index(axis_name)
    forward = [(i, (i + 1) % count) for i in range(count)]
    backward = [(i, (i - 1) % count) for i in range(count)]
    rounds = count // 2
    half = block.shape[1] // 2
    from_behind, from_ahead = [], []
    carry_ahead, carry_behind = block, block
    for step in range(1, rounds):
        carry_ahead = lax.ppermute(carry_ahead, axis_name, forward)
        carry_behind = lax.ppermute(carry_behind, axis_name, backward)
        from_behind.append(carry_ahead)
        from_ahead.append(carry_behind)
    if count % 2 == 0:
        opposite = jnp.concatenate(
            [
                lax.ppermute(carry_ahead[:, :half], axis_name, forward),
                lax.ppermute(carry_behind[:, half:], axis_name, backward),
            ],
            axis=1,
        )
        middle = [opposite]
    else:
        middle = [lax.ppermute(carry_ahead, axis_name, forward)]
        from_ahead.append(lax.ppermute(carry_behind, axis_name, backward))
    by_offset = jnp.stack([block] + from_ahead + middle + from_behind[::-1])
    placed = jnp.roll(by_offset, here, axis=0)
    return placed.reshape((count * block.shape[0],) + block.shape[1:])


def col_gather(block):
    chips = lax.axis_size("chip")
    core = lax.axis_index("core")
    spread = jnp.broadcast_to(block[None], (chips,) + block.shape)
    mine = lax.all_to_all(spread, "chip", 0, 0, tiled=True)
    other = lax.ppermute(mine, "core", [(0, 1), (1, 0)])
    paired = jnp.where(core == 0, jnp.stack([mine, other], 1), jnp.stack([other, mine], 1))
    return paired.reshape((chips * 2 * block.shape[0],) + block.shape[1:])


def col_scatter_sum(parts):
    chips = lax.axis_size("chip")
    core = lax.axis_index("core")
    pieces = parts.reshape((chips, 2, parts.shape[0] // (2 * chips)) + parts.shape[1:])
    mine = lax.dynamic_index_in_dim(pieces, core, 1, keepdims=False)
    other = lax.dynamic_index_in_dim(pieces, 1 - core, 1, keepdims=False)
    pair_sum = mine + lax.ppermute(other, "core", [(0, 1), (1, 0)])
    return lax.all_to_all(pair_sum, "chip", 0, 0, tiled=True).sum(axis=0)


def on_device(tokens, cotangent, w_gate, w_up, w_down, order_gate, order_up, order_down):
    rows_here = w_gate.shape[0] // BLOCK
    cols_here = w_gate.shape[1] // BLOCK
    row_start = lax.axis_index("row") * rows_here
    col_start = (lax.axis_index("chip") * 2 + lax.axis_index("core")) * cols_here
    width_blocks = rows_here * lax.axis_size("row")
    hidden_blocks = cols_here * lax.axis_size("chip") * 2
    hidden_here = w_gate.shape[1]
    keep_gate = kept_table(order_gate, row_start, col_start, rows_here, cols_here, hidden_blocks)
    keep_up = kept_table(order_up, row_start, col_start, rows_here, cols_here, hidden_blocks)
    keep_down = kept_table(order_down, col_start, row_start, cols_here, rows_here, width_blocks)
    width_here = tokens.shape[1]
    inputs_all = col_gather(jnp.concatenate([tokens, cotangent], axis=1))
    tokens_all, cotangent_all = inputs_all[:, :width_here], inputs_all[:, width_here:]
    gate_term = apply_blocks(tokens_all, w_gate, keep_gate, "forward")
    up_term = apply_blocks(tokens_all, w_up, keep_up, "forward")
    hidden_term = apply_blocks(cotangent_all, w_down, keep_down, "transposed")
    sums = relay_scatter_sum(jnp.concatenate([gate_term, up_term, hidden_term], axis=1), "row")
    gate = sums[:, :hidden_here]
    up = sums[:, hidden_here : 2 * hidden_here]
    hidden_grad = sums[:, 2 * hidden_here :]
    sigmoid_gate = jax.nn.sigmoid(gate)
    activation = gate * sigmoid_gate
    hidden = (activation * up).astype(jnp.bfloat16)
    gate_grad = (hidden_grad * up * sigmoid_gate * (1.0 + gate * (1.0 - sigmoid_gate))).astype(
        jnp.bfloat16
    )
    up_grad = (hidden_grad * activation).astype(jnp.bfloat16)
    acts_all = relay_gather(jnp.concatenate([hidden, gate_grad, up_grad], axis=1), "row")
    hidden_all = acts_all[:, :hidden_here]
    gate_grad_all = acts_all[:, hidden_here : 2 * hidden_here]
    up_grad_all = acts_all[:, 2 * hidden_here :]
    output_term = apply_blocks(hidden_all, w_down, keep_down, "forward")
    down_weight_grad = apply_blocks(hidden_all, cotangent_all, keep_down, "weights")
    gate_weight_grad = apply_blocks(tokens_all, gate_grad_all, keep_gate, "weights")
    up_weight_grad = apply_blocks(tokens_all, up_grad_all, keep_up, "weights")
    through_gate = apply_blocks(gate_grad_all, w_gate, keep_gate, "transposed")
    through_up = apply_blocks(up_grad_all, w_up, keep_up, "transposed")
    outs = col_scatter_sum(jnp.concatenate([output_term, through_gate + through_up], axis=1))
    output = outs[:, :width_here].astype(jnp.bfloat16)
    input_grad = outs[:, width_here:]
    return (
        output,
        input_grad.astype(jnp.bfloat16),
        gate_weight_grad,
        up_weight_grad,
        down_weight_grad,
    )


def solution(mesh):
    rows, cols = mesh.devices.shape
    split = Mesh(mesh.devices.reshape(rows, cols // 2, 2), ("row", "chip", "core"))
    col = ("chip", "core")
    placed = (
        P(col, "row"),
        P(col, "row"),
        P("row", col),
        P("row", col),
        P(col, "row"),
        P(),
        P(),
        P(),
    )
    return jax.shard_map(
        on_device,
        mesh=split,
        in_specs=placed,
        out_specs=(
            P(col, "row"),
            P(col, "row"),
            P("row", col),
            P("row", col),
            P(col, "row"),
        ),
        check_vma=False,
    )
```

```python
import jax
import jax.numpy as jnp
from jax import lax
from jax.sharding import Mesh, PartitionSpec as P

BLOCK = 256


def kept_table(order, row_first, col_first, row_count, col_count, stride):
    kept_count = order.shape[0] // 2
    row_ids = row_first + jnp.arange(row_count, dtype=jnp.int32)
    col_ids = col_first + jnp.arange(col_count, dtype=jnp.int32)
    block_ids = row_ids[:, None] * stride + col_ids[None, :]
    return jnp.any(block_ids[:, :, None] == order[:kept_count][None, None, :], axis=2)


def expand_mask(kept_mask):
    row_count, col_count = kept_mask.shape
    spread = jnp.broadcast_to(kept_mask[:, None, :, None], (row_count, BLOCK, col_count, BLOCK))
    return spread.reshape(row_count * BLOCK, col_count * BLOCK)


def dense_apply(left_operand, right_operand, kept_mask, product_kind):
    full_mask = expand_mask(kept_mask)
    if product_kind == "forward":
        masked = right_operand * full_mask.astype(right_operand.dtype)
        return jnp.dot(left_operand, masked, preferred_element_type=jnp.float32)
    if product_kind == "transposed":
        masked = right_operand * full_mask.astype(right_operand.dtype)
        return lax.dot_general(
            left_operand, masked, (((1,), (1,)), ((), ())), preferred_element_type=jnp.float32
        )
    product = lax.dot_general(
        left_operand, right_operand, (((0,), (0,)), ((), ())), preferred_element_type=jnp.float32
    )
    return product * full_mask.astype(jnp.float32)


def apply_blocks(left_operand, right_operand, kept_mask, product_kind):
    return dense_apply(left_operand, right_operand, kept_mask, product_kind)


def a2a_scatter_sum(parts, axis_name):
    count = lax.axis_size(axis_name)
    pieces = parts.reshape((count, parts.shape[0] // count) + parts.shape[1:])
    return lax.all_to_all(pieces, axis_name, 0, 0, tiled=True).sum(axis=0)


def a2a_gather(block, axis_name):
    count = lax.axis_size(axis_name)
    spread = jnp.broadcast_to(block[None], (count,) + block.shape)
    gathered = lax.all_to_all(spread, axis_name, 0, 0, tiled=True)
    return gathered.reshape((count * block.shape[0],) + block.shape[1:])


def ring_scatter_sum(parts, axis_name):
    count = lax.axis_size(axis_name)
    here = lax.axis_index(axis_name)
    pieces = parts.reshape((count, parts.shape[0] // count) + parts.shape[1:])
    half = parts.shape[1] // 2
    ahead, behind = pieces[:, :, :half], pieces[:, :, half:]
    forward = [(i, (i + 1) % count) for i in range(count)]
    backward = [(i, (i - 1) % count) for i in range(count)]
    carry_ahead = lax.dynamic_index_in_dim(ahead, (here - 1) % count, 0, keepdims=False)
    carry_behind = lax.dynamic_index_in_dim(behind, (here + 1) % count, 0, keepdims=False)
    for step in range(1, count):
        carry_ahead = lax.ppermute(carry_ahead, axis_name, forward) + lax.dynamic_index_in_dim(
            ahead, (here - 1 - step) % count, 0, keepdims=False
        )
        carry_behind = lax.ppermute(carry_behind, axis_name, backward) + lax.dynamic_index_in_dim(
            behind, (here + 1 + step) % count, 0, keepdims=False
        )
    return jnp.concatenate([carry_ahead, carry_behind], axis=1)


def joint_permute(values, axis_name, pairs):
    if len(values) == 1:
        return [lax.ppermute(values[0], axis_name, pairs)]
    widths = [v.shape[1] for v in values]
    moved = lax.ppermute(jnp.concatenate(values, axis=1), axis_name, pairs)
    edges = [sum(widths[:k]) for k in range(len(widths) + 1)]
    return [moved[:, edges[k] : edges[k + 1]] for k in range(len(values))]


def relay_scatter_sum(parts, axis_name):
    count = lax.axis_size(axis_name)
    here = lax.axis_index(axis_name)
    pieces = parts.reshape((count, parts.shape[0] // count) + parts.shape[1:])
    half = parts.shape[1] // 2
    spans = (slice(0, half), slice(half, parts.shape[1]))

    def piece_for(offset, span):
        return lax.dynamic_index_in_dim(pieces, (here + offset) % count, 0, keepdims=False)[:, span]

    forward = [(i, (i + 1) % count) for i in range(count)]
    backward = [(i, (i - 1) % count) for i in range(count)]
    longer = count // 2
    shorter = count - 1 - longer
    reach = ((longer, shorter), (shorter, longer))
    ahead = [piece_for(r[0], span) for r, span in zip(reach, spans)]
    behind = [piece_for(-r[1], span) for r, span in zip(reach, spans)]
    for step in range(1, longer + 1):
        going = [c for c, r in enumerate(reach) if step <= r[0]]
        coming = [c for c, r in enumerate(reach) if step <= r[1]]
        sent_ahead = joint_permute([ahead[c] for c in going], axis_name, forward)
        sent_behind = joint_permute([behind[c] for c in coming], axis_name, backward)
        for c, value in zip(going, sent_ahead):
            ahead[c] = value + piece_for(reach[c][0] - step, spans[c]) if step < reach[c][0] else value
        for c, value in zip(coming, sent_behind):
            behind[c] = value + piece_for(step - reach[c][1], spans[c]) if step < reach[c][1] else value
    return jnp.concatenate(
        [piece_for(0, span) + ahead[c] + behind[c] for c, span in enumerate(spans)], axis=1
    )


def relay_gather(block, axis_name):
    count = lax.axis_size(axis_name)
    here = lax.axis_index(axis_name)
    forward = [(i, (i + 1) % count) for i in range(count)]
    backward = [(i, (i - 1) % count) for i in range(count)]
    rounds = count // 2
    half = block.shape[1] // 2
    from_behind, from_ahead = [], []
    carry_ahead, carry_behind = block, block
    for step in range(1, rounds):
        carry_ahead = lax.ppermute(carry_ahead, axis_name, forward)
        carry_behind = lax.ppermute(carry_behind, axis_name, backward)
        from_behind.append(carry_ahead)
        from_ahead.append(carry_behind)
    if count % 2 == 0:
        opposite = jnp.concatenate(
            [
                lax.ppermute(carry_ahead[:, :half], axis_name, forward),
                lax.ppermute(carry_behind[:, half:], axis_name, backward),
            ],
            axis=1,
        )
        middle = [opposite]
    else:
        middle = [lax.ppermute(carry_ahead, axis_name, forward)]
        from_ahead.append(lax.ppermute(carry_behind, axis_name, backward))
    by_offset = jnp.stack([block] + from_ahead + middle + from_behind[::-1])
    placed = jnp.roll(by_offset, here, axis=0)
    return placed.reshape((count * block.shape[0],) + block.shape[1:])


def col_gather(block, groups):
    chips = lax.axis_size("chip")
    spread = jnp.broadcast_to(block[None], (chips,) + block.shape)
    mine = lax.all_to_all(spread, "chip", 0, 0, tiled=True)
    other = lax.ppermute(mine, "core", [(0, 1), (1, 0)])
    grouped = (groups, chips // groups) + block.shape
    paired = jnp.stack([mine.reshape(grouped), other.reshape(grouped)], axis=1)
    return paired.reshape((chips * 2 * block.shape[0],) + block.shape[1:])


def col_scatter_sum(parts, groups):
    chips = lax.axis_size("chip")
    rows_each = parts.shape[0] // (2 * chips)
    pieces = parts.reshape((groups, 2, chips // groups, rows_each) + parts.shape[1:])
    mine = pieces[:, 0].reshape((chips, rows_each) + parts.shape[1:])
    other = pieces[:, 1].reshape((chips, rows_each) + parts.shape[1:])
    pair_sum = mine + lax.ppermute(other, "core", [(0, 1), (1, 0)])
    return lax.all_to_all(pair_sum, "chip", 0, 0, tiled=True).sum(axis=0)


def on_device(tokens, cotangent, w_gate, w_up, w_down, order_gate, order_up, order_down):
    rows_here = w_gate.shape[0] // BLOCK
    cols_here = w_gate.shape[1] // BLOCK
    row_start = lax.axis_index("row") * rows_here
    col_start = (lax.axis_index("chip") * 2 + lax.axis_index("core")) * cols_here
    width_blocks = rows_here * lax.axis_size("row")
    hidden_blocks = cols_here * lax.axis_size("chip") * 2
    hidden_here = w_gate.shape[1]
    keep_gate = kept_table(order_gate, row_start, col_start, rows_here, cols_here, hidden_blocks)
    keep_up = kept_table(order_up, row_start, col_start, rows_here, cols_here, hidden_blocks)
    keep_down = kept_table(order_down, col_start, row_start, cols_here, rows_here, width_blocks)
    width_here = tokens.shape[1]
    groups = lax.axis_size("row")
    inputs_all = col_gather(jnp.concatenate([tokens, cotangent], axis=1), groups)
    tokens_all, cotangent_all = inputs_all[:, :width_here], inputs_all[:, width_here:]
    gate_term = apply_blocks(tokens_all, w_gate, keep_gate, "forward")
    up_term = apply_blocks(tokens_all, w_up, keep_up, "forward")
    hidden_term = apply_blocks(cotangent_all, w_down, keep_down, "transposed")
    sums = relay_scatter_sum(jnp.concatenate([gate_term, up_term, hidden_term], axis=1), "row")
    gate = sums[:, :hidden_here]
    up = sums[:, hidden_here : 2 * hidden_here]
    hidden_grad = sums[:, 2 * hidden_here :]
    sigmoid_gate = jax.nn.sigmoid(gate)
    activation = gate * sigmoid_gate
    hidden = (activation * up).astype(jnp.bfloat16)
    gate_grad = (hidden_grad * up * sigmoid_gate * (1.0 + gate * (1.0 - sigmoid_gate))).astype(
        jnp.bfloat16
    )
    up_grad = (hidden_grad * activation).astype(jnp.bfloat16)
    acts_all = relay_gather(jnp.concatenate([hidden, gate_grad, up_grad], axis=1), "row")
    hidden_all = acts_all[:, :hidden_here]
    gate_grad_all = acts_all[:, hidden_here : 2 * hidden_here]
    up_grad_all = acts_all[:, 2 * hidden_here :]
    output_term = apply_blocks(hidden_all, w_down, keep_down, "forward")
    down_weight_grad = apply_blocks(hidden_all, cotangent_all, keep_down, "weights")
    gate_weight_grad = apply_blocks(tokens_all, gate_grad_all, keep_gate, "weights")
    up_weight_grad = apply_blocks(tokens_all, up_grad_all, keep_up, "weights")
    through_gate = apply_blocks(gate_grad_all, w_gate, keep_gate, "transposed")
    through_up = apply_blocks(up_grad_all, w_up, keep_up, "transposed")
    outs = col_scatter_sum(jnp.concatenate([output_term, through_gate + through_up], axis=1), groups)
    output = outs[:, :width_here].astype(jnp.bfloat16)
    input_grad = outs[:, width_here:]
    return (
        output,
        input_grad.astype(jnp.bfloat16),
        gate_weight_grad,
        up_weight_grad,
        down_weight_grad,
    )


def solution(mesh):
    rows, cols = mesh.devices.shape
    split = Mesh(mesh.devices.reshape(rows, cols // 2, 2), ("row", "chip", "core"))
    col = ("chip", "core")
    placed = (
        P(col, "row"),
        P(col, "row"),
        P("row", col),
        P("row", col),
        P(col, "row"),
        P(),
        P(),
        P(),
    )
    return jax.shard_map(
        on_device,
        mesh=split,
        in_specs=placed,
        out_specs=(
            P(col, "row"),
            P(col, "row"),
            P("row", col),
            P("row", col),
            P(col, "row"),
        ),
        check_vma=False,
    )
```

```python
import jax
import jax.numpy as jnp
from jax import lax
from jax.experimental.layout import Layout, with_layout_constraint
from jax.sharding import Mesh, PartitionSpec as P

BLOCK = 256


def kept_table(order, row_first, col_first, row_count, col_count, stride):
    kept_count = order.shape[0] // 2
    row_ids = row_first + jnp.arange(row_count, dtype=jnp.int32)
    col_ids = col_first + jnp.arange(col_count, dtype=jnp.int32)
    block_ids = row_ids[:, None] * stride + col_ids[None, :]
    return jnp.any(block_ids[:, :, None] == order[:kept_count][None, None, :], axis=2)


def expand_mask(kept_mask):
    row_count, col_count = kept_mask.shape
    spread = jnp.broadcast_to(kept_mask[:, None, :, None], (row_count, BLOCK, col_count, BLOCK))
    return spread.reshape(row_count * BLOCK, col_count * BLOCK)


def dense_apply(left_operand, right_operand, kept_mask, product_kind):
    full_mask = expand_mask(kept_mask)
    if product_kind == "forward":
        masked = right_operand * full_mask.astype(right_operand.dtype)
        return jnp.dot(left_operand, masked, preferred_element_type=jnp.float32)
    if product_kind == "transposed":
        masked = right_operand * full_mask.astype(right_operand.dtype)
        return lax.dot_general(
            left_operand, masked, (((1,), (1,)), ((), ())), preferred_element_type=jnp.float32
        )
    product = lax.dot_general(
        left_operand, right_operand, (((0,), (0,)), ((), ())), preferred_element_type=jnp.float32
    )
    return product * full_mask.astype(jnp.float32)


def apply_blocks(left_operand, right_operand, kept_mask, product_kind):
    return dense_apply(left_operand, right_operand, kept_mask, product_kind)


def a2a_scatter_sum(parts, axis_name):
    count = lax.axis_size(axis_name)
    pieces = parts.reshape((count, parts.shape[0] // count) + parts.shape[1:])
    return lax.all_to_all(pieces, axis_name, 0, 0, tiled=True).sum(axis=0)


def a2a_gather(block, axis_name):
    count = lax.axis_size(axis_name)
    spread = jnp.broadcast_to(block[None], (count,) + block.shape)
    gathered = lax.all_to_all(spread, axis_name, 0, 0, tiled=True)
    return gathered.reshape((count * block.shape[0],) + block.shape[1:])


def ring_scatter_sum(parts, axis_name):
    count = lax.axis_size(axis_name)
    here = lax.axis_index(axis_name)
    pieces = parts.reshape((count, parts.shape[0] // count) + parts.shape[1:])
    half = parts.shape[1] // 2
    ahead, behind = pieces[:, :, :half], pieces[:, :, half:]
    forward = [(i, (i + 1) % count) for i in range(count)]
    backward = [(i, (i - 1) % count) for i in range(count)]
    carry_ahead = lax.dynamic_index_in_dim(ahead, (here - 1) % count, 0, keepdims=False)
    carry_behind = lax.dynamic_index_in_dim(behind, (here + 1) % count, 0, keepdims=False)
    for step in range(1, count):
        carry_ahead = lax.ppermute(carry_ahead, axis_name, forward) + lax.dynamic_index_in_dim(
            ahead, (here - 1 - step) % count, 0, keepdims=False
        )
        carry_behind = lax.ppermute(carry_behind, axis_name, backward) + lax.dynamic_index_in_dim(
            behind, (here + 1 + step) % count, 0, keepdims=False
        )
    return jnp.concatenate([carry_ahead, carry_behind], axis=1)


def joint_permute(values, axis_name, pairs):
    if len(values) == 1:
        return [lax.ppermute(values[0], axis_name, pairs)]
    widths = [v.shape[1] for v in values]
    moved = lax.ppermute(jnp.concatenate(values, axis=1), axis_name, pairs)
    edges = [sum(widths[:k]) for k in range(len(widths) + 1)]
    return [moved[:, edges[k] : edges[k + 1]] for k in range(len(values))]


def relay_scatter_sum(parts, axis_name):
    count = lax.axis_size(axis_name)
    here = lax.axis_index(axis_name)
    pieces = parts.reshape((count, parts.shape[0] // count) + parts.shape[1:])
    half = parts.shape[1] // 2
    spans = (slice(0, half), slice(half, parts.shape[1]))

    def piece_for(offset, span):
        return lax.dynamic_index_in_dim(pieces, (here + offset) % count, 0, keepdims=False)[:, span]

    forward = [(i, (i + 1) % count) for i in range(count)]
    backward = [(i, (i - 1) % count) for i in range(count)]
    longer = count // 2
    shorter = count - 1 - longer
    reach = ((longer, shorter), (shorter, longer))
    ahead = [piece_for(r[0], span) for r, span in zip(reach, spans)]
    behind = [piece_for(-r[1], span) for r, span in zip(reach, spans)]
    for step in range(1, longer + 1):
        going = [c for c, r in enumerate(reach) if step <= r[0]]
        coming = [c for c, r in enumerate(reach) if step <= r[1]]
        sent_ahead = joint_permute([ahead[c] for c in going], axis_name, forward)
        sent_behind = joint_permute([behind[c] for c in coming], axis_name, backward)
        for c, value in zip(going, sent_ahead):
            ahead[c] = value + piece_for(reach[c][0] - step, spans[c]) if step < reach[c][0] else value
        for c, value in zip(coming, sent_behind):
            behind[c] = value + piece_for(step - reach[c][1], spans[c]) if step < reach[c][1] else value
    return jnp.concatenate(
        [piece_for(0, span) + ahead[c] + behind[c] for c, span in enumerate(spans)], axis=1
    )


def relay_gather(block, axis_name):
    count = lax.axis_size(axis_name)
    here = lax.axis_index(axis_name)
    forward = [(i, (i + 1) % count) for i in range(count)]
    backward = [(i, (i - 1) % count) for i in range(count)]
    rounds = count // 2
    half = block.shape[1] // 2
    from_behind, from_ahead = [], []
    carry_ahead, carry_behind = block, block
    for step in range(1, rounds):
        carry_ahead = lax.ppermute(carry_ahead, axis_name, forward)
        carry_behind = lax.ppermute(carry_behind, axis_name, backward)
        from_behind.append(carry_ahead)
        from_ahead.append(carry_behind)
    if count % 2 == 0:
        opposite = jnp.concatenate(
            [
                lax.ppermute(carry_ahead[:, :half], axis_name, forward),
                lax.ppermute(carry_behind[:, half:], axis_name, backward),
            ],
            axis=1,
        )
        middle = [opposite]
    else:
        middle = [lax.ppermute(carry_ahead, axis_name, forward)]
        from_ahead.append(lax.ppermute(carry_behind, axis_name, backward))
    by_offset = jnp.stack([block] + from_ahead + middle + from_behind[::-1])
    placed = jnp.roll(by_offset, here, axis=0)
    return placed.reshape((count * block.shape[0],) + block.shape[1:])


def col_gather(block, groups):
    chips = lax.axis_size("chip")
    spread = jnp.broadcast_to(block[None], (chips,) + block.shape)
    mine = lax.all_to_all(spread, "chip", 0, 0, tiled=True)
    other = lax.ppermute(mine, "core", [(0, 1), (1, 0)])
    grouped = (groups, chips // groups) + block.shape
    paired = jnp.stack([mine.reshape(grouped), other.reshape(grouped)], axis=1)
    return paired.reshape((chips * 2 * block.shape[0],) + block.shape[1:])


def col_scatter_sum(parts, groups):
    chips = lax.axis_size("chip")
    rows_each = parts.shape[0] // (2 * chips)
    pieces = parts.reshape((groups, 2, chips // groups, rows_each) + parts.shape[1:])
    mine = pieces[:, 0].reshape((chips, rows_each) + parts.shape[1:])
    other = pieces[:, 1].reshape((chips, rows_each) + parts.shape[1:])
    pair_sum = mine + lax.ppermute(other, "core", [(0, 1), (1, 0)])
    return lax.all_to_all(pair_sum, "chip", 0, 0, tiled=True).sum(axis=0)


def on_device(tokens, cotangent, w_gate, w_up, w_down, order_gate, order_up, order_down):
    rows_here = w_gate.shape[0] // BLOCK
    cols_here = w_gate.shape[1] // BLOCK
    row_start = lax.axis_index("row") * rows_here
    col_start = (lax.axis_index("chip") * 2 + lax.axis_index("core")) * cols_here
    width_blocks = rows_here * lax.axis_size("row")
    hidden_blocks = cols_here * lax.axis_size("chip") * 2
    hidden_here = w_gate.shape[1]
    keep_gate = kept_table(order_gate, row_start, col_start, rows_here, cols_here, hidden_blocks)
    keep_up = kept_table(order_up, row_start, col_start, rows_here, cols_here, hidden_blocks)
    keep_down = kept_table(order_down, col_start, row_start, cols_here, rows_here, width_blocks)
    width_here = tokens.shape[1]
    groups = lax.axis_size("row")
    inputs_all = col_gather(jnp.concatenate([tokens, cotangent], axis=1), groups)
    tokens_all, cotangent_all = inputs_all[:, :width_here], inputs_all[:, width_here:]
    gate_term = apply_blocks(tokens_all, w_gate, keep_gate, "forward")
    up_term = apply_blocks(tokens_all, w_up, keep_up, "forward")
    hidden_term = apply_blocks(cotangent_all, w_down, keep_down, "transposed")
    row_major = Layout(major_to_minor=(0, 1))
    partials = [with_layout_constraint(t, row_major) for t in (gate_term, up_term, hidden_term)]
    sums = relay_scatter_sum(jnp.concatenate(partials, axis=1), "row")
    gate = sums[:, :hidden_here]
    up = sums[:, hidden_here : 2 * hidden_here]
    hidden_grad = sums[:, 2 * hidden_here :]
    sigmoid_gate = jax.nn.sigmoid(gate)
    activation = gate * sigmoid_gate
    hidden = (activation * up).astype(jnp.bfloat16)
    gate_grad = (hidden_grad * up * sigmoid_gate * (1.0 + gate * (1.0 - sigmoid_gate))).astype(
        jnp.bfloat16
    )
    up_grad = (hidden_grad * activation).astype(jnp.bfloat16)
    acts_all = relay_gather(jnp.concatenate([hidden, gate_grad, up_grad], axis=1), "row")
    hidden_all = acts_all[:, :hidden_here]
    gate_grad_all = acts_all[:, hidden_here : 2 * hidden_here]
    up_grad_all = acts_all[:, 2 * hidden_here :]
    output_term = apply_blocks(hidden_all, w_down, keep_down, "forward")
    down_weight_grad = apply_blocks(hidden_all, cotangent_all, keep_down, "weights")
    gate_weight_grad = apply_blocks(tokens_all, gate_grad_all, keep_gate, "weights")
    up_weight_grad = apply_blocks(tokens_all, up_grad_all, keep_up, "weights")
    through_gate = apply_blocks(gate_grad_all, w_gate, keep_gate, "transposed")
    through_up = apply_blocks(up_grad_all, w_up, keep_up, "transposed")
    outs = col_scatter_sum(jnp.concatenate([output_term, through_gate + through_up], axis=1), groups)
    output = outs[:, :width_here].astype(jnp.bfloat16)
    input_grad = outs[:, width_here:]
    return (
        output,
        input_grad.astype(jnp.bfloat16),
        gate_weight_grad,
        up_weight_grad,
        down_weight_grad,
    )


def solution(mesh):
    rows, cols = mesh.devices.shape
    split = Mesh(mesh.devices.reshape(rows, cols // 2, 2), ("row", "chip", "core"))
    col = ("chip", "core")
    placed = (
        P(col, "row"),
        P(col, "row"),
        P("row", col),
        P("row", col),
        P(col, "row"),
        P(),
        P(),
        P(),
    )
    return jax.shard_map(
        on_device,
        mesh=split,
        in_specs=placed,
        out_specs=(
            P(col, "row"),
            P(col, "row"),
            P("row", col),
            P("row", col),
            P(col, "row"),
        ),
        check_vma=False,
    )
```

```python
import jax
import jax.numpy as jnp
from jax import lax
from jax.experimental.layout import Layout, with_layout_constraint
from jax.sharding import Mesh, PartitionSpec as P

BLOCK = 256


def kept_table(order, row_first, col_first, row_count, col_count, stride):
    kept_count = order.shape[0] // 2
    row_ids = row_first + jnp.arange(row_count, dtype=jnp.int32)
    col_ids = col_first + jnp.arange(col_count, dtype=jnp.int32)
    block_ids = row_ids[:, None] * stride + col_ids[None, :]
    return jnp.any(block_ids[:, :, None] == order[:kept_count][None, None, :], axis=2)


def expand_mask(kept_mask):
    row_count, col_count = kept_mask.shape
    spread = jnp.broadcast_to(kept_mask[:, None, :, None], (row_count, BLOCK, col_count, BLOCK))
    return spread.reshape(row_count * BLOCK, col_count * BLOCK)


def dense_apply(left_operand, right_operand, kept_mask, product_kind):
    full_mask = expand_mask(kept_mask)
    if product_kind == "forward":
        masked = right_operand * full_mask.astype(right_operand.dtype)
        return jnp.dot(left_operand, masked, preferred_element_type=jnp.float32)
    if product_kind == "transposed":
        masked = right_operand * full_mask.astype(right_operand.dtype)
        return lax.dot_general(
            left_operand, masked, (((1,), (1,)), ((), ())), preferred_element_type=jnp.float32
        )
    product = lax.dot_general(
        left_operand, right_operand, (((0,), (0,)), ((), ())), preferred_element_type=jnp.float32
    )
    return product * full_mask.astype(jnp.float32)


def apply_blocks(left_operand, right_operand, kept_mask, product_kind):
    return dense_apply(left_operand, right_operand, kept_mask, product_kind)


def a2a_scatter_sum(parts, axis_name):
    count = lax.axis_size(axis_name)
    pieces = parts.reshape((count, parts.shape[0] // count) + parts.shape[1:])
    return lax.all_to_all(pieces, axis_name, 0, 0, tiled=True).sum(axis=0)


def a2a_gather(block, axis_name):
    count = lax.axis_size(axis_name)
    spread = jnp.broadcast_to(block[None], (count,) + block.shape)
    gathered = lax.all_to_all(spread, axis_name, 0, 0, tiled=True)
    return gathered.reshape((count * block.shape[0],) + block.shape[1:])


def ring_scatter_sum(parts, axis_name):
    count = lax.axis_size(axis_name)
    here = lax.axis_index(axis_name)
    pieces = parts.reshape((count, parts.shape[0] // count) + parts.shape[1:])
    half = parts.shape[1] // 2
    ahead, behind = pieces[:, :, :half], pieces[:, :, half:]
    forward = [(i, (i + 1) % count) for i in range(count)]
    backward = [(i, (i - 1) % count) for i in range(count)]
    carry_ahead = lax.dynamic_index_in_dim(ahead, (here - 1) % count, 0, keepdims=False)
    carry_behind = lax.dynamic_index_in_dim(behind, (here + 1) % count, 0, keepdims=False)
    for step in range(1, count):
        carry_ahead = lax.ppermute(carry_ahead, axis_name, forward) + lax.dynamic_index_in_dim(
            ahead, (here - 1 - step) % count, 0, keepdims=False
        )
        carry_behind = lax.ppermute(carry_behind, axis_name, backward) + lax.dynamic_index_in_dim(
            behind, (here + 1 + step) % count, 0, keepdims=False
        )
    return jnp.concatenate([carry_ahead, carry_behind], axis=1)


def joint_permute(values, axis_name, pairs):
    if len(values) == 1:
        return [lax.ppermute(values[0], axis_name, pairs)]
    widths = [v.shape[1] for v in values]
    moved = lax.ppermute(jnp.concatenate(values, axis=1), axis_name, pairs)
    edges = [sum(widths[:k]) for k in range(len(widths) + 1)]
    return [moved[:, edges[k] : edges[k + 1]] for k in range(len(values))]


def relay_scatter_sum(chains, axis_name):
    count = lax.axis_size(axis_name)
    here = lax.axis_index(axis_name)
    split = [
        (part.reshape((count, part.shape[0] // count) + part.shape[1:]), reach)
        for part, reach in chains
    ]

    def piece_for(c, offset):
        return lax.dynamic_index_in_dim(split[c][0], (here + offset) % count, 0, keepdims=False)

    forward = [(i, (i + 1) % count) for i in range(count)]
    backward = [(i, (i - 1) % count) for i in range(count)]
    reach = [r for _, r in split]
    ahead = [piece_for(c, r[0]) for c, r in enumerate(reach)]
    behind = [piece_for(c, -r[1]) for c, r in enumerate(reach)]
    for step in range(1, max(max(r) for r in reach) + 1):
        going = [c for c, r in enumerate(reach) if step <= r[0]]
        coming = [c for c, r in enumerate(reach) if step <= r[1]]
        sent_ahead = joint_permute([ahead[c] for c in going], axis_name, forward)
        sent_behind = joint_permute([behind[c] for c in coming], axis_name, backward)
        for c, value in zip(going, sent_ahead):
            ahead[c] = value + piece_for(c, reach[c][0] - step) if step < reach[c][0] else value
        for c, value in zip(coming, sent_behind):
            behind[c] = value + piece_for(c, step - reach[c][1]) if step < reach[c][1] else value
    return [piece_for(c, 0) + ahead[c] + behind[c] for c in range(len(split))]


def relay_gather(block, axis_name):
    count = lax.axis_size(axis_name)
    here = lax.axis_index(axis_name)
    forward = [(i, (i + 1) % count) for i in range(count)]
    backward = [(i, (i - 1) % count) for i in range(count)]
    rounds = count // 2
    half = block.shape[1] // 2
    from_behind, from_ahead = [], []
    carry_ahead, carry_behind = block, block
    for step in range(1, rounds):
        carry_ahead = lax.ppermute(carry_ahead, axis_name, forward)
        carry_behind = lax.ppermute(carry_behind, axis_name, backward)
        from_behind.append(carry_ahead)
        from_ahead.append(carry_behind)
    if count % 2 == 0:
        opposite = jnp.concatenate(
            [
                lax.ppermute(carry_ahead[:, :half], axis_name, forward),
                lax.ppermute(carry_behind[:, half:], axis_name, backward),
            ],
            axis=1,
        )
        middle = [opposite]
    else:
        middle = [lax.ppermute(carry_ahead, axis_name, forward)]
        from_ahead.append(lax.ppermute(carry_behind, axis_name, backward))
    by_offset = jnp.stack([block] + from_ahead + middle + from_behind[::-1])
    placed = jnp.roll(by_offset, here, axis=0)
    return placed.reshape((count * block.shape[0],) + block.shape[1:])


def col_gather(block, groups):
    chips = lax.axis_size("chip")
    spread = jnp.broadcast_to(block[None], (chips,) + block.shape)
    mine = lax.all_to_all(spread, "chip", 0, 0, tiled=True)
    other = lax.ppermute(mine, "core", [(0, 1), (1, 0)])
    grouped = (groups, chips // groups) + block.shape
    paired = jnp.stack([mine.reshape(grouped), other.reshape(grouped)], axis=1)
    return paired.reshape((chips * 2 * block.shape[0],) + block.shape[1:])


def col_scatter_sum(parts, groups):
    chips = lax.axis_size("chip")
    rows_each = parts.shape[0] // (2 * chips)
    pieces = parts.reshape((groups, 2, chips // groups, rows_each) + parts.shape[1:])
    mine = pieces[:, 0].reshape((chips, rows_each) + parts.shape[1:])
    other = pieces[:, 1].reshape((chips, rows_each) + parts.shape[1:])
    pair_sum = mine + lax.ppermute(other, "core", [(0, 1), (1, 0)])
    return lax.all_to_all(pair_sum, "chip", 0, 0, tiled=True).sum(axis=0)


def on_device(tokens, cotangent, w_gate, w_up, w_down, order_gate, order_up, order_down):
    rows_here = w_gate.shape[0] // BLOCK
    cols_here = w_gate.shape[1] // BLOCK
    row_start = lax.axis_index("row") * rows_here
    col_start = (lax.axis_index("chip") * 2 + lax.axis_index("core")) * cols_here
    width_blocks = rows_here * lax.axis_size("row")
    hidden_blocks = cols_here * lax.axis_size("chip") * 2
    hidden_here = w_gate.shape[1]
    keep_gate = kept_table(order_gate, row_start, col_start, rows_here, cols_here, hidden_blocks)
    keep_up = kept_table(order_up, row_start, col_start, rows_here, cols_here, hidden_blocks)
    keep_down = kept_table(order_down, col_start, row_start, cols_here, rows_here, width_blocks)
    width_here = tokens.shape[1]
    groups = lax.axis_size("row")
    inputs_all = col_gather(jnp.concatenate([tokens, cotangent], axis=1), groups)
    tokens_all, cotangent_all = inputs_all[:, :width_here], inputs_all[:, width_here:]
    gate_term = apply_blocks(tokens_all, w_gate, keep_gate, "forward")
    up_term = apply_blocks(tokens_all, w_up, keep_up, "forward")
    hidden_term = apply_blocks(cotangent_all, w_down, keep_down, "transposed")
    row_major = Layout(major_to_minor=(0, 1))
    gate_term, up_term, hidden_term = (
        with_layout_constraint(t, row_major) for t in (gate_term, up_term, hidden_term)
    )
    groups_row = lax.axis_size("row")
    longer = groups_row // 2
    shorter = groups_row - 1 - longer
    half_up = hidden_here // 2
    gate, up_first, up_second, hidden_grad = relay_scatter_sum(
        [
            (gate_term, (longer, shorter)),
            (up_term[:, :half_up], (longer, shorter)),
            (up_term[:, half_up:], (shorter, longer)),
            (hidden_term, (shorter, longer)),
        ],
        "row",
    )
    up = jnp.concatenate([up_first, up_second], axis=1)
    sigmoid_gate = jax.nn.sigmoid(gate)
    activation = gate * sigmoid_gate
    hidden = (activation * up).astype(jnp.bfloat16)
    gate_grad = (hidden_grad * up * sigmoid_gate * (1.0 + gate * (1.0 - sigmoid_gate))).astype(
        jnp.bfloat16
    )
    up_grad = (hidden_grad * activation).astype(jnp.bfloat16)
    acts_all = relay_gather(jnp.concatenate([hidden, gate_grad, up_grad], axis=1), "row")
    hidden_all = acts_all[:, :hidden_here]
    gate_grad_all = acts_all[:, hidden_here : 2 * hidden_here]
    up_grad_all = acts_all[:, 2 * hidden_here :]
    output_term = apply_blocks(hidden_all, w_down, keep_down, "forward")
    down_weight_grad = apply_blocks(hidden_all, cotangent_all, keep_down, "weights")
    gate_weight_grad = apply_blocks(tokens_all, gate_grad_all, keep_gate, "weights")
    up_weight_grad = apply_blocks(tokens_all, up_grad_all, keep_up, "weights")
    through_gate = apply_blocks(gate_grad_all, w_gate, keep_gate, "transposed")
    through_up = apply_blocks(up_grad_all, w_up, keep_up, "transposed")
    outs = col_scatter_sum(jnp.concatenate([output_term, through_gate + through_up], axis=1), groups)
    output = outs[:, :width_here].astype(jnp.bfloat16)
    input_grad = outs[:, width_here:]
    return (
        output,
        input_grad.astype(jnp.bfloat16),
        gate_weight_grad,
        up_weight_grad,
        down_weight_grad,
    )


def solution(mesh):
    rows, cols = mesh.devices.shape
    split = Mesh(mesh.devices.reshape(rows, cols // 2, 2), ("row", "chip", "core"))
    col = ("chip", "core")
    placed = (
        P(col, "row"),
        P(col, "row"),
        P("row", col),
        P("row", col),
        P(col, "row"),
        P(),
        P(),
        P(),
    )
    return jax.shard_map(
        on_device,
        mesh=split,
        in_specs=placed,
        out_specs=(
            P(col, "row"),
            P(col, "row"),
            P("row", col),
            P("row", col),
            P(col, "row"),
        ),
        check_vma=False,
    )
```

```python
import jax
import jax.numpy as jnp
from jax import lax
from jax.experimental.layout import Layout, with_layout_constraint
from jax.sharding import Mesh, PartitionSpec as P

BLOCK = 256


def kept_table(order, row_first, col_first, row_count, col_count, stride):
    kept_count = order.shape[0] // 2
    row_ids = row_first + jnp.arange(row_count, dtype=jnp.int32)
    col_ids = col_first + jnp.arange(col_count, dtype=jnp.int32)
    block_ids = row_ids[:, None] * stride + col_ids[None, :]
    return jnp.any(block_ids[:, :, None] == order[:kept_count][None, None, :], axis=2)


def expand_mask(kept_mask):
    row_count, col_count = kept_mask.shape
    spread = jnp.broadcast_to(kept_mask[:, None, :, None], (row_count, BLOCK, col_count, BLOCK))
    return spread.reshape(row_count * BLOCK, col_count * BLOCK)


def dense_apply(left_operand, right_operand, kept_mask, product_kind):
    full_mask = expand_mask(kept_mask)
    if product_kind == "forward":
        masked = right_operand * full_mask.astype(right_operand.dtype)
        return jnp.dot(left_operand, masked, preferred_element_type=jnp.float32)
    if product_kind == "transposed":
        masked = right_operand * full_mask.astype(right_operand.dtype)
        return lax.dot_general(
            left_operand, masked, (((1,), (1,)), ((), ())), preferred_element_type=jnp.float32
        )
    product = lax.dot_general(
        left_operand, right_operand, (((0,), (0,)), ((), ())), preferred_element_type=jnp.float32
    )
    return product * full_mask.astype(jnp.float32)


def apply_blocks(left_operand, right_operand, kept_mask, product_kind):
    return dense_apply(left_operand, right_operand, kept_mask, product_kind)


def a2a_scatter_sum(parts, axis_name):
    count = lax.axis_size(axis_name)
    pieces = parts.reshape((count, parts.shape[0] // count) + parts.shape[1:])
    return lax.all_to_all(pieces, axis_name, 0, 0, tiled=True).sum(axis=0)


def a2a_gather(block, axis_name):
    count = lax.axis_size(axis_name)
    spread = jnp.broadcast_to(block[None], (count,) + block.shape)
    gathered = lax.all_to_all(spread, axis_name, 0, 0, tiled=True)
    return gathered.reshape((count * block.shape[0],) + block.shape[1:])


def ring_scatter_sum(parts, axis_name):
    count = lax.axis_size(axis_name)
    here = lax.axis_index(axis_name)
    pieces = parts.reshape((count, parts.shape[0] // count) + parts.shape[1:])
    half = parts.shape[1] // 2
    ahead, behind = pieces[:, :, :half], pieces[:, :, half:]
    forward = [(i, (i + 1) % count) for i in range(count)]
    backward = [(i, (i - 1) % count) for i in range(count)]
    carry_ahead = lax.dynamic_index_in_dim(ahead, (here - 1) % count, 0, keepdims=False)
    carry_behind = lax.dynamic_index_in_dim(behind, (here + 1) % count, 0, keepdims=False)
    for step in range(1, count):
        carry_ahead = lax.ppermute(carry_ahead, axis_name, forward) + lax.dynamic_index_in_dim(
            ahead, (here - 1 - step) % count, 0, keepdims=False
        )
        carry_behind = lax.ppermute(carry_behind, axis_name, backward) + lax.dynamic_index_in_dim(
            behind, (here + 1 + step) % count, 0, keepdims=False
        )
    return jnp.concatenate([carry_ahead, carry_behind], axis=1)


def joint_permute(values, axis_name, pairs):
    if len(values) == 1:
        return [lax.ppermute(values[0], axis_name, pairs)]
    widths = [v.shape[1] for v in values]
    moved = lax.ppermute(jnp.concatenate(values, axis=1), axis_name, pairs)
    edges = [sum(widths[:k]) for k in range(len(widths) + 1)]
    return [moved[:, edges[k] : edges[k + 1]] for k in range(len(values))]


def relay_scatter_sum(parts, axis_name):
    count = lax.axis_size(axis_name)
    here = lax.axis_index(axis_name)
    pieces = parts.reshape((count, parts.shape[0] // count) + parts.shape[1:])
    half = parts.shape[1] // 2
    spans = (slice(0, half), slice(half, parts.shape[1]))

    def piece_for(offset, span):
        return lax.dynamic_index_in_dim(pieces, (here + offset) % count, 0, keepdims=False)[:, span]

    forward = [(i, (i + 1) % count) for i in range(count)]
    backward = [(i, (i - 1) % count) for i in range(count)]
    longer = count // 2
    shorter = count - 1 - longer
    reach = ((longer, shorter), (shorter, longer))
    ahead = [piece_for(r[0], span) for r, span in zip(reach, spans)]
    behind = [piece_for(-r[1], span) for r, span in zip(reach, spans)]
    for step in range(1, longer + 1):
        going = [c for c, r in enumerate(reach) if step <= r[0]]
        coming = [c for c, r in enumerate(reach) if step <= r[1]]
        sent_ahead = joint_permute([ahead[c] for c in going], axis_name, forward)
        sent_behind = joint_permute([behind[c] for c in coming], axis_name, backward)
        for c, value in zip(going, sent_ahead):
            ahead[c] = value + piece_for(reach[c][0] - step, spans[c]) if step < reach[c][0] else value
        for c, value in zip(coming, sent_behind):
            behind[c] = value + piece_for(step - reach[c][1], spans[c]) if step < reach[c][1] else value
    return jnp.concatenate(
        [piece_for(0, span) + ahead[c] + behind[c] for c, span in enumerate(spans)], axis=1
    )


def relay_gather(block, axis_name):
    count = lax.axis_size(axis_name)
    here = lax.axis_index(axis_name)
    forward = [(i, (i + 1) % count) for i in range(count)]
    backward = [(i, (i - 1) % count) for i in range(count)]
    rounds = count // 2
    half = block.shape[1] // 2
    from_behind, from_ahead = [], []
    carry_ahead, carry_behind = block, block
    for step in range(1, rounds):
        carry_ahead = lax.ppermute(carry_ahead, axis_name, forward)
        carry_behind = lax.ppermute(carry_behind, axis_name, backward)
        from_behind.append(carry_ahead)
        from_ahead.append(carry_behind)
    if count % 2 == 0:
        opposite = jnp.concatenate(
            [
                lax.ppermute(carry_ahead[:, :half], axis_name, forward),
                lax.ppermute(carry_behind[:, half:], axis_name, backward),
            ],
            axis=1,
        )
        middle = [opposite]
    else:
        middle = [lax.ppermute(carry_ahead, axis_name, forward)]
        from_ahead.append(lax.ppermute(carry_behind, axis_name, backward))
    by_offset = jnp.stack([block] + from_ahead + middle + from_behind[::-1])
    placed = jnp.roll(by_offset, here, axis=0)
    return placed.reshape((count * block.shape[0],) + block.shape[1:])


def col_gather(block, groups):
    chips = lax.axis_size("chip")
    spread = jnp.broadcast_to(block[None], (chips,) + block.shape)
    mine = lax.all_to_all(spread, "chip", 0, 0, tiled=True)
    other = lax.ppermute(mine, "core", [(0, 1), (1, 0)])
    grouped = (groups, chips // groups) + block.shape
    paired = jnp.stack([mine.reshape(grouped), other.reshape(grouped)], axis=1)
    return paired.reshape((chips * 2 * block.shape[0],) + block.shape[1:])


def col_scatter_sum(mine_part, other_part):
    chips = lax.axis_size("chip")
    shape = (chips, mine_part.shape[0] // chips) + mine_part.shape[1:]
    swapped = lax.ppermute(other_part.reshape(shape), "core", [(0, 1), (1, 0)])
    pair_sum = mine_part.reshape(shape) + swapped
    return lax.all_to_all(pair_sum, "chip", 0, 0, tiled=True).sum(axis=0)


def on_device(tokens, cotangent, w_gate, w_up, w_down, order_gate, order_up, order_down):
    rows_here = w_gate.shape[0] // BLOCK
    cols_here = w_gate.shape[1] // BLOCK
    row_start = lax.axis_index("row") * rows_here
    col_start = (lax.axis_index("chip") * 2 + lax.axis_index("core")) * cols_here
    width_blocks = rows_here * lax.axis_size("row")
    hidden_blocks = cols_here * lax.axis_size("chip") * 2
    hidden_here = w_gate.shape[1]
    keep_gate = kept_table(order_gate, row_start, col_start, rows_here, cols_here, hidden_blocks)
    keep_up = kept_table(order_up, row_start, col_start, rows_here, cols_here, hidden_blocks)
    keep_down = kept_table(order_down, col_start, row_start, cols_here, rows_here, width_blocks)
    width_here = tokens.shape[1]
    groups = lax.axis_size("row")
    inputs_all = col_gather(jnp.concatenate([tokens, cotangent], axis=1), groups)
    tokens_all, cotangent_all = inputs_all[:, :width_here], inputs_all[:, width_here:]
    gate_term = apply_blocks(tokens_all, w_gate, keep_gate, "forward")
    up_term = apply_blocks(tokens_all, w_up, keep_up, "forward")
    hidden_term = apply_blocks(cotangent_all, w_down, keep_down, "transposed")
    row_major = Layout(major_to_minor=(0, 1))
    partials = [with_layout_constraint(t, row_major) for t in (gate_term, up_term, hidden_term)]
    sums = relay_scatter_sum(jnp.concatenate(partials, axis=1), "row")
    gate = sums[:, :hidden_here]
    up = sums[:, hidden_here : 2 * hidden_here]
    hidden_grad = sums[:, 2 * hidden_here :]
    sigmoid_gate = jax.nn.sigmoid(gate)
    activation = gate * sigmoid_gate
    hidden = (activation * up).astype(jnp.bfloat16)
    gate_grad = (hidden_grad * up * sigmoid_gate * (1.0 + gate * (1.0 - sigmoid_gate))).astype(
        jnp.bfloat16
    )
    up_grad = (hidden_grad * activation).astype(jnp.bfloat16)
    acts_all = relay_gather(jnp.concatenate([hidden, gate_grad, up_grad], axis=1), "row")
    hidden_all = acts_all[:, :hidden_here]
    gate_grad_all = acts_all[:, hidden_here : 2 * hidden_here]
    up_grad_all = acts_all[:, 2 * hidden_here :]
    down_weight_grad = apply_blocks(hidden_all, cotangent_all, keep_down, "weights")
    gate_weight_grad = apply_blocks(tokens_all, gate_grad_all, keep_gate, "weights")
    up_weight_grad = apply_blocks(tokens_all, up_grad_all, keep_up, "weights")
    by_core = acts_all.reshape((groups, 2, -1) + acts_all.shape[1:])

    def sum_terms(rows):
        rows = rows.reshape((-1,) + acts_all.shape[1:])
        output_term = apply_blocks(rows[:, :hidden_here], w_down, keep_down, "forward")
        through_gate = apply_blocks(rows[:, hidden_here : 2 * hidden_here], w_gate, keep_gate, "transposed")
        through_up = apply_blocks(rows[:, 2 * hidden_here :], w_up, keep_up, "transposed")
        return jnp.concatenate([output_term, through_gate + through_up], axis=1)

    outs = col_scatter_sum(sum_terms(by_core[:, 0]), sum_terms(by_core[:, 1]))
    output = outs[:, :width_here].astype(jnp.bfloat16)
    input_grad = outs[:, width_here:]
    return (
        output,
        input_grad.astype(jnp.bfloat16),
        gate_weight_grad,
        up_weight_grad,
        down_weight_grad,
    )


def solution(mesh):
    rows, cols = mesh.devices.shape
    split = Mesh(mesh.devices.reshape(rows, cols // 2, 2), ("row", "chip", "core"))
    col = ("chip", "core")
    placed = (
        P(col, "row"),
        P(col, "row"),
        P("row", col),
        P("row", col),
        P(col, "row"),
        P(),
        P(),
        P(),
    )
    return jax.shard_map(
        on_device,
        mesh=split,
        in_specs=placed,
        out_specs=(
            P(col, "row"),
            P(col, "row"),
            P("row", col),
            P("row", col),
            P(col, "row"),
        ),
        check_vma=False,
    )
```

```python
import jax
import jax.numpy as jnp
from jax import lax
from jax.experimental.layout import Layout, with_layout_constraint
from jax.sharding import Mesh, PartitionSpec as P

BLOCK = 256


def kept_table(order, row_first, col_first, row_count, col_count, stride):
    kept_count = order.shape[0] // 2
    row_ids = row_first + jnp.arange(row_count, dtype=jnp.int32)
    col_ids = col_first + jnp.arange(col_count, dtype=jnp.int32)
    block_ids = row_ids[:, None] * stride + col_ids[None, :]
    return jnp.any(block_ids[:, :, None] == order[:kept_count][None, None, :], axis=2)


def expand_mask(kept_mask):
    row_count, col_count = kept_mask.shape
    spread = jnp.broadcast_to(kept_mask[:, None, :, None], (row_count, BLOCK, col_count, BLOCK))
    return spread.reshape(row_count * BLOCK, col_count * BLOCK)


def dense_apply(left_operand, right_operand, kept_mask, product_kind):
    full_mask = expand_mask(kept_mask)
    if product_kind == "forward":
        masked = right_operand * full_mask.astype(right_operand.dtype)
        return jnp.dot(left_operand, masked, preferred_element_type=jnp.float32)
    if product_kind == "transposed":
        masked = right_operand * full_mask.astype(right_operand.dtype)
        return lax.dot_general(
            left_operand, masked, (((1,), (1,)), ((), ())), preferred_element_type=jnp.float32
        )
    product = lax.dot_general(
        left_operand, right_operand, (((0,), (0,)), ((), ())), preferred_element_type=jnp.float32
    )
    return product * full_mask.astype(jnp.float32)


def apply_blocks(left_operand, right_operand, kept_mask, product_kind):
    return dense_apply(left_operand, right_operand, kept_mask, product_kind)


def a2a_scatter_sum(parts, axis_name):
    count = lax.axis_size(axis_name)
    pieces = parts.reshape((count, parts.shape[0] // count) + parts.shape[1:])
    return lax.all_to_all(pieces, axis_name, 0, 0, tiled=True).sum(axis=0)


def a2a_gather(block, axis_name):
    count = lax.axis_size(axis_name)
    spread = jnp.broadcast_to(block[None], (count,) + block.shape)
    gathered = lax.all_to_all(spread, axis_name, 0, 0, tiled=True)
    return gathered.reshape((count * block.shape[0],) + block.shape[1:])


def ring_scatter_sum(parts, axis_name):
    count = lax.axis_size(axis_name)
    here = lax.axis_index(axis_name)
    pieces = parts.reshape((count, parts.shape[0] // count) + parts.shape[1:])
    half = parts.shape[1] // 2
    ahead, behind = pieces[:, :, :half], pieces[:, :, half:]
    forward = [(i, (i + 1) % count) for i in range(count)]
    backward = [(i, (i - 1) % count) for i in range(count)]
    carry_ahead = lax.dynamic_index_in_dim(ahead, (here - 1) % count, 0, keepdims=False)
    carry_behind = lax.dynamic_index_in_dim(behind, (here + 1) % count, 0, keepdims=False)
    for step in range(1, count):
        carry_ahead = lax.ppermute(carry_ahead, axis_name, forward) + lax.dynamic_index_in_dim(
            ahead, (here - 1 - step) % count, 0, keepdims=False
        )
        carry_behind = lax.ppermute(carry_behind, axis_name, backward) + lax.dynamic_index_in_dim(
            behind, (here + 1 + step) % count, 0, keepdims=False
        )
    return jnp.concatenate([carry_ahead, carry_behind], axis=1)


def joint_permute(values, axis_name, pairs):
    if len(values) == 1:
        return [lax.ppermute(values[0], axis_name, pairs)]
    widths = [v.shape[1] for v in values]
    moved = lax.ppermute(jnp.concatenate(values, axis=1), axis_name, pairs)
    edges = [sum(widths[:k]) for k in range(len(widths) + 1)]
    return [moved[:, edges[k] : edges[k + 1]] for k in range(len(values))]


def relay_scatter_sum(parts, axis_name):
    count = lax.axis_size(axis_name)
    here = lax.axis_index(axis_name)
    pieces = parts.reshape((count, parts.shape[0] // count) + parts.shape[1:])
    half = parts.shape[1] // 2
    spans = (slice(0, half), slice(half, parts.shape[1]))

    def piece_for(offset, span):
        return lax.dynamic_index_in_dim(pieces, (here + offset) % count, 0, keepdims=False)[:, span]

    forward = [(i, (i + 1) % count) for i in range(count)]
    backward = [(i, (i - 1) % count) for i in range(count)]
    longer = count // 2
    shorter = count - 1 - longer
    reach = ((longer, shorter), (shorter, longer))
    ahead = [piece_for(r[0], span) for r, span in zip(reach, spans)]
    behind = [piece_for(-r[1], span) for r, span in zip(reach, spans)]
    for step in range(1, longer + 1):
        going = [c for c, r in enumerate(reach) if step <= r[0]]
        coming = [c for c, r in enumerate(reach) if step <= r[1]]
        sent_ahead = joint_permute([ahead[c] for c in going], axis_name, forward)
        sent_behind = joint_permute([behind[c] for c in coming], axis_name, backward)
        for c, value in zip(going, sent_ahead):
            ahead[c] = value + piece_for(reach[c][0] - step, spans[c]) if step < reach[c][0] else value
        for c, value in zip(coming, sent_behind):
            behind[c] = value + piece_for(step - reach[c][1], spans[c]) if step < reach[c][1] else value
    return jnp.concatenate(
        [piece_for(0, span) + ahead[c] + behind[c] for c, span in enumerate(spans)], axis=1
    )


def relay_gather(block, axis_name):
    count = lax.axis_size(axis_name)
    here = lax.axis_index(axis_name)
    forward = [(i, (i + 1) % count) for i in range(count)]
    backward = [(i, (i - 1) % count) for i in range(count)]
    rounds = count // 2
    half = block.shape[1] // 2
    from_behind, from_ahead = [], []
    carry_ahead, carry_behind = block, block
    for step in range(1, rounds):
        carry_ahead = lax.ppermute(carry_ahead, axis_name, forward)
        carry_behind = lax.ppermute(carry_behind, axis_name, backward)
        from_behind.append(carry_ahead)
        from_ahead.append(carry_behind)
    if count % 2 == 0:
        opposite = jnp.concatenate(
            [
                lax.ppermute(carry_ahead[:, :half], axis_name, forward),
                lax.ppermute(carry_behind[:, half:], axis_name, backward),
            ],
            axis=1,
        )
        middle = [opposite]
    else:
        middle = [lax.ppermute(carry_ahead, axis_name, forward)]
        from_ahead.append(lax.ppermute(carry_behind, axis_name, backward))
    by_offset = jnp.stack([block] + from_ahead + middle + from_behind[::-1])
    placed = jnp.roll(by_offset, here, axis=0)
    return placed.reshape((count * block.shape[0],) + block.shape[1:])


def col_gather(block, groups):
    chips = lax.axis_size("chip")
    spread = jnp.broadcast_to(block[None], (chips,) + block.shape)
    mine = lax.all_to_all(spread, "chip", 0, 0, tiled=True)
    other = lax.ppermute(mine, "core", [(0, 1), (1, 0)])
    return mine, other


def col_scatter_sum(mine_part, other_part):
    chips = lax.axis_size("chip")
    shape = (chips, mine_part.shape[0] // chips) + mine_part.shape[1:]
    swapped = lax.ppermute(other_part.reshape(shape), "core", [(0, 1), (1, 0)])
    pair_sum = mine_part.reshape(shape) + swapped
    return lax.all_to_all(pair_sum, "chip", 0, 0, tiled=True).sum(axis=0)


def on_device(tokens, cotangent, w_gate, w_up, w_down, order_gate, order_up, order_down):
    rows_here = w_gate.shape[0] // BLOCK
    cols_here = w_gate.shape[1] // BLOCK
    row_start = lax.axis_index("row") * rows_here
    col_start = (lax.axis_index("chip") * 2 + lax.axis_index("core")) * cols_here
    width_blocks = rows_here * lax.axis_size("row")
    hidden_blocks = cols_here * lax.axis_size("chip") * 2
    hidden_here = w_gate.shape[1]
    keep_gate = kept_table(order_gate, row_start, col_start, rows_here, cols_here, hidden_blocks)
    keep_up = kept_table(order_up, row_start, col_start, rows_here, cols_here, hidden_blocks)
    keep_down = kept_table(order_down, col_start, row_start, cols_here, rows_here, width_blocks)
    width_here = tokens.shape[1]
    groups = lax.axis_size("row")
    halves = col_gather(jnp.concatenate([tokens, cotangent], axis=1), groups)
    grouped = (groups, 1, -1) + halves[0].shape[2:]
    inputs_all = jnp.concatenate([h.reshape(grouped) for h in halves], axis=1)
    inputs_all = inputs_all.reshape((-1,) + halves[0].shape[2:])
    tokens_all, cotangent_all = inputs_all[:, :width_here], inputs_all[:, width_here:]
    row_major = Layout(major_to_minor=(0, 1))

    def partial_terms(half):
        rows = half.reshape((-1,) + half.shape[2:])
        terms = (
            apply_blocks(rows[:, :width_here], w_gate, keep_gate, "forward"),
            apply_blocks(rows[:, :width_here], w_up, keep_up, "forward"),
            apply_blocks(rows[:, width_here:], w_down, keep_down, "transposed"),
        )
        joined = jnp.concatenate([with_layout_constraint(t, row_major) for t in terms], axis=1)
        return joined.reshape((groups, 1, -1) + joined.shape[1:])

    partial = jnp.concatenate([partial_terms(h) for h in halves], axis=1)
    partials = [partial.reshape((-1,) + partial.shape[3:])]
    sums = relay_scatter_sum(jnp.concatenate(partials, axis=1), "row")
    gate = sums[:, :hidden_here]
    up = sums[:, hidden_here : 2 * hidden_here]
    hidden_grad = sums[:, 2 * hidden_here :]
    sigmoid_gate = jax.nn.sigmoid(gate)
    activation = gate * sigmoid_gate
    hidden = (activation * up).astype(jnp.bfloat16)
    gate_grad = (hidden_grad * up * sigmoid_gate * (1.0 + gate * (1.0 - sigmoid_gate))).astype(
        jnp.bfloat16
    )
    up_grad = (hidden_grad * activation).astype(jnp.bfloat16)
    acts_all = relay_gather(jnp.concatenate([hidden, gate_grad, up_grad], axis=1), "row")
    hidden_all = acts_all[:, :hidden_here]
    gate_grad_all = acts_all[:, hidden_here : 2 * hidden_here]
    up_grad_all = acts_all[:, 2 * hidden_here :]
    down_weight_grad = apply_blocks(hidden_all, cotangent_all, keep_down, "weights")
    gate_weight_grad = apply_blocks(tokens_all, gate_grad_all, keep_gate, "weights")
    up_weight_grad = apply_blocks(tokens_all, up_grad_all, keep_up, "weights")
    by_core = acts_all.reshape((groups, 2, -1) + acts_all.shape[1:])

    def sum_terms(rows):
        rows = rows.reshape((-1,) + acts_all.shape[1:])
        output_term = apply_blocks(rows[:, :hidden_here], w_down, keep_down, "forward")
        through_gate = apply_blocks(rows[:, hidden_here : 2 * hidden_here], w_gate, keep_gate, "transposed")
        through_up = apply_blocks(rows[:, 2 * hidden_here :], w_up, keep_up, "transposed")
        return jnp.concatenate([output_term, through_gate + through_up], axis=1)

    outs = col_scatter_sum(sum_terms(by_core[:, 0]), sum_terms(by_core[:, 1]))
    output = outs[:, :width_here].astype(jnp.bfloat16)
    input_grad = outs[:, width_here:]
    return (
        output,
        input_grad.astype(jnp.bfloat16),
        gate_weight_grad,
        up_weight_grad,
        down_weight_grad,
    )


def solution(mesh):
    rows, cols = mesh.devices.shape
    split = Mesh(mesh.devices.reshape(rows, cols // 2, 2), ("row", "chip", "core"))
    col = ("chip", "core")
    placed = (
        P(col, "row"),
        P(col, "row"),
        P("row", col),
        P("row", col),
        P(col, "row"),
        P(),
        P(),
        P(),
    )
    return jax.shard_map(
        on_device,
        mesh=split,
        in_specs=placed,
        out_specs=(
            P(col, "row"),
            P(col, "row"),
            P("row", col),
            P("row", col),
            P(col, "row"),
        ),
        check_vma=False,
    )
```
